512 devices in a mesh: gx: 16 (over x_hi, z), gy: 32 (over y, x_lo, core).
Axes of the slice: x: 4 (x_hi: 2, x_lo: 2; x = x_hi * 2 + x_lo), y: 8, z: 8, core: 2. Of those that a mesh axis runs over, the one named last changes fastest.
Arguments:
- features: bfloat16 [16, 32, 16, 256], P('gx', 'gy'), may hold values from -6 to 6
- atom_kinds: int32 [16, 32, 16], P('gx', 'gy'), may hold values from 0 to 1
- kind_table: float32 [2, 256], replicated, may hold values from -6 to 6
- band_vectors: bfloat16 [16, 32, 16, 13, 32], P('gx', 'gy'), may hold values from -6 to 6
- pair_offsets: float32 [16, 32, 3, 9, 128], P('gx', 'gy'), may hold values from -7 to 7, as said below
- pair_source: int32 [16, 32, 9, 128], P('gx', 'gy'), may hold values from 0 to 15
- pair_target: int32 [16, 32, 9, 128], P('gx', 'gy'), may hold values from 0 to 15
- pair_live_mask: int32 [16, 32, 9, 128], P('gx', 'gy'), may hold values from 0 to 1, as said below
- radial_weight: bfloat16 [16, 256], replicated, may hold values from -1.5 to 1.5
- w_source: bfloat16 [256, 256], replicated, may hold values from -0.375 to 0.375
- w_target: bfloat16 [256, 256], replicated, may hold values from -0.375 to 0.375
- mixing_weight: bfloat16 [256, 256], replicated, may hold values from -0.375 to 0.375
- gate_weight: bfloat16 [256, 256], replicated, may hold values from -0.375 to 0.375
- output_weight: bfloat16 [256, 169], replicated, may hold values from -0.375 to 0.375
- w_site: bfloat16 [256, 169], replicated, may hold values from -0.375 to 0.375
Outputs:
- filtered: float32 [16, 32, 16, 13, 32], P('gx', 'gy')
The draws below stay inside these ranges and needn't reach their ends.
Inputs may be any that keep to these rules, and one draw needn't show every extreme that they name: `pair_offsets`: the length of every offset lies between 1.2 and 8. `pair_live_mask`: the share of live slots differs from block to block.
All inputs are finite; a program needn't handle non-finite values.
Results may differ from the reference program's by a relative error of at most 0.007.
Values may be sent and summed in bfloat16 or wider, within the bound.
No kernel may reach another device: no remote copies, remote signals or barrier semaphores. Data moves between devices by JAX's collectives and lax.ppermute only.
A program may use at most 64 MiB of HBM per device.

```python
import math
import jax
import jax.numpy as jnp
from jax import lax

ATOMS = 16
NEIGHBOUR_SLOTS = 72
BLOCK_PAIR_SLOTS = 128
FEAT = 256
RBF = 16
ORBITAL_COUNT = 13
VEC = 32
KINDS = 2
FILTER = 3
BLOCKS_X = 16
BLOCKS_Y = 32


def draw_pair_offsets(key, part):
    key_radius, key_angle, key_height = jax.random.split(key, 3)
    shape = (BLOCKS_X, BLOCKS_Y, 9, BLOCK_PAIR_SLOTS)
    radius = jax.random.uniform(key_radius, shape, dtype=jnp.float32, minval=1.2, maxval=7.0)
    angle = jax.random.uniform(key_angle, shape, dtype=jnp.float32, minval=-math.pi, maxval=math.pi)
    height = jax.random.uniform(key_height, shape, dtype=jnp.float32, minval=-3.6, maxval=3.6)
    return jnp.stack([radius * jnp.cos(angle), radius * jnp.sin(angle), height], axis=2).astype(jnp.float32)


def draw_pair_live_mask(key, part):
    key_level, key_slot = jax.random.split(key, 2)
    level = jax.random.randint(key_level, (BLOCKS_X, BLOCKS_Y, 1, 1), 1, 5)
    level = level.at[0, 0].set(4)
    level = level.at[BLOCKS_X - 1, BLOCKS_Y - 1].set(1)
    ticket = jax.random.randint(key_slot, (BLOCKS_X, BLOCKS_Y, 9, BLOCK_PAIR_SLOTS), 0, 4)
    return (ticket < level).astype(jnp.int32)


def place_ends(result, rng, least, largest):
    spot = [jax.random.randint(jax.random.fold_in(rng, axis), (), 0, length) for axis, length in enumerate(result.shape)]
    main_axis = result.shape.index(max(result.shape))
    next_to = spot[:main_axis] + [(spot[main_axis] + 1) % result.shape[main_axis]] + spot[main_axis + 1:]
    return result.at[tuple(spot)].set(least).at[tuple(next_to)].set(largest)


def block_levels(rng, shape, pieces, smallest, top_value):
    def one(axis_at, shards_of):
        heights = jax.random.uniform(jax.random.fold_in(jax.random.fold_in(rng, 6), axis_at), (shards_of,), jnp.float32, smallest / len(pieces), top_value / len(pieces))
        return jnp.repeat(jnp.exp(heights), shape[axis_at] // shards_of).reshape((-1,) + (1,) * (len(shape) - axis_at - 1))

    loudness = one(*pieces[0])
    for cut in pieces[1:]:
        loudness = loudness * one(*cut)
    return loudness


def bell_draw(rng, dims, deviation, limit, cuts=(), kind=jnp.bfloat16):
    loudness = block_levels(rng, dims, cuts, -0.22, 0.18) if cuts else 1.0
    values = jax.random.normal(rng, dims, jnp.float32) * deviation * loudness
    return jnp.minimum(jnp.maximum(values, -limit), limit).astype(kind)


def setup_inputs(seed: int = 0) -> dict:
    keys = jax.random.split(jax.random.key(seed), 16)
    features = bell_draw(keys[0], (BLOCKS_X, BLOCKS_Y, ATOMS, FEAT), 1.0, 6.0, ((0, 16), (1, 32)))
    atom_kinds = place_ends(jax.random.randint(keys[1], (BLOCKS_X, BLOCKS_Y, ATOMS), 0, KINDS), jax.random.fold_in(keys[1], 1), 0, KINDS - 1).astype(jnp.int32)
    kind_table = bell_draw(keys[2], (KINDS, FEAT), 1.0, 6.0, (), jnp.float32)
    band_vectors = bell_draw(keys[3], (BLOCKS_X, BLOCKS_Y, ATOMS, ORBITAL_COUNT, VEC), 1.0, 6.0, ((0, 16), (1, 32)))
    pair_offsets = draw_pair_offsets(jax.random.fold_in(keys[15], 71), 0)
    pair_source = place_ends(jax.random.randint(keys[5], (BLOCKS_X, BLOCKS_Y, 9, BLOCK_PAIR_SLOTS), 0, ATOMS), jax.random.fold_in(keys[5], 1), 0, ATOMS - 1).astype(jnp.int32)
    pair_target = place_ends(jax.random.randint(keys[6], (BLOCKS_X, BLOCKS_Y, 9, BLOCK_PAIR_SLOTS), 0, ATOMS), jax.random.fold_in(keys[6], 1), 0, ATOMS - 1).astype(jnp.int32)
    pair_live_mask = draw_pair_live_mask(jax.random.fold_in(keys[15], 71), 0)
    radial_weight = bell_draw(keys[8], (RBF, FEAT), RBF ** -0.5, 1.5)
    w_source = bell_draw(keys[9], (FEAT, FEAT), FEAT ** -0.5, 0.375)
    w_target = bell_draw(keys[10], (FEAT, FEAT), FEAT ** -0.5, 0.375)
    mixing_weight = bell_draw(keys[11], (FEAT, FEAT), FEAT ** -0.5, 0.375)
    gate_weight = bell_draw(keys[12], (FEAT, FEAT), FEAT ** -0.5, 0.375)
    output_weight = bell_draw(keys[13], (FEAT, ORBITAL_COUNT * ORBITAL_COUNT), FEAT ** -0.5, 0.375)
    w_site = bell_draw(keys[14], (FEAT, ORBITAL_COUNT * ORBITAL_COUNT), FEAT ** -0.5, 0.375)
    return dict(features=features, atom_kinds=atom_kinds, kind_table=kind_table, band_vectors=band_vectors, pair_offsets=pair_offsets, pair_source=pair_source, pair_target=pair_target, pair_live_mask=pair_live_mask, radial_weight=radial_weight, w_source=w_source, w_target=w_target, mixing_weight=mixing_weight, gate_weight=gate_weight, output_weight=output_weight, w_site=w_site)


cutoff = 8.0
onsite_scale = 0.15

def radial(block_offsets):
    distance = jnp.sqrt(block_offsets[0] * block_offsets[0] + block_offsets[1] * block_offsets[1] + block_offsets[2] * block_offsets[2])
    centres = cutoff * jnp.arange(RBF, dtype=jnp.float32) / (RBF - 1)
    spacing = cutoff / (RBF - 1)
    basis = jnp.exp(-jnp.square((distance[:, None] - centres[None, :]) / spacing)).astype(jnp.bfloat16)
    cutoff_envelope = jnp.square(1.0 - jnp.square(distance / cutoff))
    return (basis, cutoff_envelope)

def pair_block_matrices(source_atom_rows, target_atom_rows, block_offsets, live_flags, radial_weight, mixing_weight, gate_weight, output_weight):
    basis, cutoff_envelope = radial(block_offsets)
    before = source_atom_rows + target_atom_rows + jnp.dot(basis, radial_weight, preferred_element_type=jnp.float32)
    edge = jax.nn.silu(before).astype(jnp.bfloat16)
    opened = jax.nn.silu(jnp.dot(edge, mixing_weight, preferred_element_type=jnp.float32))
    mixed = (opened * jnp.dot(edge, gate_weight, preferred_element_type=jnp.float32)).astype(jnp.bfloat16)
    raw_out = jnp.dot(mixed, output_weight, preferred_element_type=jnp.float32)
    scale_factor = 1.5 / math.sqrt(NEIGHBOUR_SLOTS * ORBITAL_COUNT) * cutoff_envelope * live_flags
    return (raw_out * scale_factor[:, None]).astype(jnp.bfloat16)

def onsite_blocks(atoms, w_site):
    square = jnp.dot(atoms, w_site, preferred_element_type=jnp.float32).reshape(-1, ORBITAL_COUNT, ORBITAL_COUNT)
    return (onsite_scale * 0.5 * (square + jnp.swapaxes(square, 1, 2))).astype(jnp.bfloat16)

def reference(features, atom_kinds, kind_table, band_vectors, pair_offsets, pair_source, pair_target, pair_live_mask, radial_weight, w_source, w_target, mixing_weight, gate_weight, output_weight, w_site):
    pair_tally = BLOCKS_X * BLOCKS_Y
    kind_hot = (atom_kinds[..., None] == jnp.arange(KINDS, dtype=jnp.int32)).astype(jnp.float32)
    embedded = jnp.einsum('xyak,kf->xyaf', kind_hot, kind_table, precision=lax.Precision.HIGHEST)
    atoms = (features.astype(jnp.float32) + embedded).astype(jnp.bfloat16).reshape(pair_tally * ATOMS, FEAT)
    source_projection = jnp.dot(atoms, w_source, preferred_element_type=jnp.float32)
    target_projection = jnp.dot(atoms, w_target, preferred_element_type=jnp.float32)
    onsite = onsite_blocks(atoms, w_site)
    block_ids = jnp.arange(pair_tally, dtype=jnp.int32)
    column_id = block_ids // BLOCKS_Y
    row_id = block_ids % BLOCKS_Y
    order = jnp.arange(9, dtype=jnp.int32)
    near = (column_id[:, None] + order[None, :] // 3 - 1) % BLOCKS_X * BLOCKS_Y + (row_id[:, None] + order[None, :] % 3 - 1) % BLOCKS_Y
    global_source = (block_ids[:, None, None] * ATOMS + pair_source.reshape(pair_tally, 9, BLOCK_PAIR_SLOTS)).reshape(pair_tally, 9 * BLOCK_PAIR_SLOTS)
    global_target = (near[:, :, None] * ATOMS + pair_target.reshape(pair_tally, 9, BLOCK_PAIR_SLOTS)).reshape(pair_tally, 9 * BLOCK_PAIR_SLOTS)
    live_flags = pair_live_mask.reshape(pair_tally, 9 * BLOCK_PAIR_SLOTS)
    block_offsets = pair_offsets.reshape(pair_tally, 3, 9 * BLOCK_PAIR_SLOTS)

    def apply(vector_rows):
        vector_rows = lax.optimization_barrier(vector_rows)
        wide = vector_rows.astype(jnp.float32)

        def visit(summed, block_tile):
            source_indices = global_source[block_tile]
            target_indices = global_target[block_tile]
            hopping_block = pair_block_matrices(source_projection[source_indices], target_projection[target_indices], block_offsets[block_tile], live_flags[block_tile].astype(jnp.float32), radial_weight, mixing_weight, gate_weight, output_weight)
            matrices = hopping_block.reshape(-1, ORBITAL_COUNT, ORBITAL_COUNT).astype(jnp.float32)
            forward = jnp.einsum('poq,pqv->pov', matrices, wide[target_indices])
            backward = jnp.einsum('poq,pov->pqv', matrices, wide[source_indices])
            return (summed.at[source_indices].add(forward).at[target_indices].add(backward), None)
        start = jnp.einsum('aoq,aqv->aov', onsite.astype(jnp.float32), wide)
        summed, _ = lax.scan(visit, start, block_ids)
        return summed
    first = band_vectors.reshape(pair_tally * ATOMS, ORBITAL_COUNT, VEC)
    previous = first.astype(jnp.float32)
    current = apply(first)
    for repeat in range(FILTER - 1):
        upcoming = 2.0 * apply(current.astype(jnp.bfloat16)) - previous
        previous, current = (current, upcoming)
    return current.reshape(BLOCKS_X, BLOCKS_Y, ATOMS, ORBITAL_COUNT, VEC)
```

```python
import math

import jax
import jax.numpy as jnp
from jax import lax
from jax.sharding import PartitionSpec as P

NEIGHBOUR_SLOTS = 72
RBF = 16
ORBITAL_COUNT = 13
FILTER = 3


cutoff = 8.0
onsite_scale = 0.15

f32 = jnp.float32
bf16 = jnp.bfloat16


def shifted(value, axis, steps):
    count = lax.axis_size(axis)
    pairs = [(source, (source + steps) % count) for source in range(count)]
    return lax.ppermute(value, axis, pairs)


def bf16_parts(value):
    high = lax.reduce_precision(value, exponent_bits=8, mantissa_bits=7)
    rest = value - high
    middle = lax.reduce_precision(rest, exponent_bits=8, mantissa_bits=7)
    low = rest - middle
    return high.astype(bf16), middle.astype(bf16), low.astype(bf16)


def halo(flat):
    from_west = shifted(flat, "gx", 1)
    from_east = shifted(flat, "gx", -1)
    strip = jnp.stack([from_west, flat, from_east]).reshape(-1)
    from_south = shifted(strip, "gy", 1).reshape(3, -1)
    from_north = shifted(strip, "gy", -1).reshape(3, -1)
    strip = strip.reshape(3, -1)
    return jnp.stack([from_south, strip, from_north], axis=1).reshape(9, -1)


def first_halo(common, pairs):
    n = common.shape[0]
    m = pairs.shape[1]
    to_east = jnp.concatenate([common, pairs[6:9].reshape(-1)])
    to_west = jnp.concatenate([common, pairs[0:3].reshape(-1)])
    from_west = shifted(to_east, "gx", 1)
    from_east = shifted(to_west, "gx", -1)
    strip_common = jnp.stack([from_west[:n], common, from_east[:n]])
    strip_pairs = jnp.stack(
        [
            from_west[n:].reshape(3, m),
            pairs[3:6],
            from_east[n:].reshape(3, m),
        ]
    )
    to_north = jnp.concatenate([strip_common.reshape(-1), strip_pairs[:, 2].reshape(-1)])
    to_south = jnp.concatenate([strip_common.reshape(-1), strip_pairs[:, 0].reshape(-1)])
    from_south = shifted(to_north, "gy", 1)
    from_north = shifted(to_south, "gy", -1)
    all_common = jnp.stack(
        [from_south[: 3 * n].reshape(3, n), strip_common, from_north[: 3 * n].reshape(3, n)],
        axis=1,
    ).reshape(9, n)
    incoming = jnp.stack(
        [
            from_south[3 * n :].reshape(3, m),
            strip_pairs[:, 1],
            from_north[3 * n :].reshape(3, m),
        ],
        axis=1,
    ).reshape(9, m)
    return all_common, incoming


def pair_blocks(before_rows, distance, live_flags, radial_weight, mixing_weight, gate_weight, output_weight):
    centres = cutoff * jnp.arange(RBF, dtype=f32) / (RBF - 1)
    spacing = cutoff / (RBF - 1)
    basis = jnp.exp(-jnp.square((distance[:, None] - centres[None, :]) / spacing)).astype(bf16)
    cutoff_envelope = jnp.square(1.0 - jnp.square(distance / cutoff))
    before = before_rows + jnp.dot(basis, radial_weight, preferred_element_type=f32)
    edge = jax.nn.silu(before).astype(bf16)
    opened = jax.nn.silu(jnp.dot(edge, mixing_weight, preferred_element_type=f32))
    mixed = (opened * jnp.dot(edge, gate_weight, preferred_element_type=f32)).astype(bf16)
    raw_out = jnp.dot(mixed, output_weight, preferred_element_type=f32)
    scale_factor = 1.5 / math.sqrt(NEIGHBOUR_SLOTS * ORBITAL_COUNT) * cutoff_envelope * live_flags
    return (raw_out * scale_factor[:, None]).astype(bf16)


def on_device(
    features,
    atom_kinds,
    kind_table,
    band_vectors,
    pair_offsets,
    pair_source,
    pair_target,
    pair_live_mask,
    radial_weight,
    w_source,
    w_target,
    mixing_weight,
    gate_weight,
    output_weight,
    w_site,
):
    atom_count = features.shape[2]
    feat = features.shape[3]
    vec = band_vectors.shape[4]
    orb = ORBITAL_COUNT
    slots = pair_source.shape[3]
    kind_hot = (
        atom_kinds[0, 0][:, None] == jnp.arange(kind_table.shape[0], dtype=jnp.int32)[None, :]
    ).astype(f32)
    embedded = jnp.dot(kind_hot, kind_table, precision=lax.Precision.HIGHEST)
    atoms = (features[0, 0].astype(f32) + embedded).astype(bf16)

    offsets = pair_offsets[0, 0]
    distance = jnp.sqrt(offsets[0] * offsets[0] + offsets[1] * offsets[1] + offsets[2] * offsets[2])
    source = pair_source[0, 0]
    target = pair_target[0, 0]
    live = pair_live_mask[0, 0]
    high, middle, low = bf16_parts(distance)
    pair_data = jnp.stack(
        [source.astype(bf16), target.astype(bf16), live.astype(bf16), high, middle, low], axis=-1
    ).reshape(9, slots * 6)

    first = band_vectors[0, 0]
    common = jnp.concatenate([atoms.reshape(-1), first.reshape(-1)])
    all_common, incoming = first_halo(common, pair_data)
    n_atoms = atom_count * feat
    ring_atoms = all_common[:, :n_atoms].reshape(9 * atom_count, feat)
    ring_first = all_common[:, n_atoms:]

    incoming = incoming.reshape(9, slots, 6).astype(f32)
    in_source = incoming[..., 0].astype(jnp.int32)
    in_target = incoming[..., 1].astype(jnp.int32)
    in_live = incoming[..., 2]
    in_distance = (incoming[..., 3] + incoming[..., 4]) + incoming[..., 5]

    places = jnp.arange(9, dtype=jnp.int32)[:, None] * atom_count
    centre = 4 * atom_count
    row_source = jnp.concatenate([(centre + source).reshape(-1), (places + in_source).reshape(-1)])
    row_target = jnp.concatenate([(places + target).reshape(-1), (centre + in_target).reshape(-1)])
    all_distance = jnp.concatenate([distance.reshape(-1), in_distance.reshape(-1)])
    all_live = jnp.concatenate([live.reshape(-1).astype(f32), in_live.reshape(-1)])

    source_projection = jnp.dot(ring_atoms, w_source, preferred_element_type=f32)
    target_projection = jnp.dot(ring_atoms, w_target, preferred_element_type=f32)
    table = jnp.concatenate([source_projection, target_projection])
    table_parts = jnp.concatenate(bf16_parts(table), axis=1)
    ring = 9 * atom_count
    columns = jnp.arange(2 * ring, dtype=jnp.int32)[None, :]
    pick = (
        (columns == row_source[:, None]) | (columns == (row_target[:, None] + ring))
    ).astype(bf16)
    picked = jnp.dot(pick, table_parts, preferred_element_type=f32)
    before_rows = (picked[:, :feat] + picked[:, feat : 2 * feat]) + picked[:, 2 * feat :]

    hopping = pair_blocks(
        before_rows, all_distance, all_live, radial_weight, mixing_weight, gate_weight, output_weight
    )
    own_hopping = hopping[: 9 * slots].reshape(9, slots, orb * orb)
    in_hopping = jnp.swapaxes(
        hopping[9 * slots :].reshape(9, slots, orb, orb), 2, 3
    ).reshape(9, slots, orb * orb)

    pair_ids = jnp.arange(atom_count * atom_count, dtype=jnp.int32)[None, None, :]
    own_key = source * atom_count + target
    in_key = in_target * atom_count + in_source
    own_hot = (own_key[:, :, None] == pair_ids).astype(bf16)
    in_hot = (in_key[:, :, None] == pair_ids).astype(bf16)
    summed = jnp.einsum("tsp,tsb->tpb", own_hot, own_hopping, preferred_element_type=f32)
    summed = summed + jnp.einsum("tsp,tsb->tpb", in_hot, in_hopping, preferred_element_type=f32)

    square = jnp.dot(atoms, w_site, preferred_element_type=f32).reshape(-1, orb, orb)
    onsite = (onsite_scale * 0.5 * (square + jnp.swapaxes(square, 1, 2))).astype(bf16)
    eye = jnp.eye(atom_count, dtype=f32)
    onsite_full = (eye[:, :, None, None] * onsite.astype(f32)[:, None, :, :]).reshape(
        atom_count * atom_count, orb * orb
    )
    summed = summed.at[4].add(onsite_full)
    dense = jnp.transpose(
        summed.reshape(9, atom_count, atom_count, orb, orb), (1, 3, 0, 2, 4)
    ).reshape(atom_count * orb, 9 * atom_count * orb)

    def apply(ring_vectors):
        wide = ring_vectors.reshape(9 * atom_count * orb, vec).astype(f32)
        out = jnp.dot(dense, wide, precision=lax.Precision.HIGHEST, preferred_element_type=f32)
        return out.reshape(atom_count, orb, vec)

    previous = first.astype(f32)
    current = apply(ring_first)
    for repeat in range(FILTER - 1):
        ring_now = halo(current.astype(bf16).reshape(-1))
        upcoming = 2.0 * apply(ring_now) - previous
        previous, current = (current, upcoming)
    return current[None, None]


def solution(mesh):
    in_specs = (
        P("gx", "gy", None, None),
        P("gx", "gy", None),
        P(),
        P("gx", "gy", None, None, None),
        P("gx", "gy", None, None, None),
        P("gx", "gy", None, None),
        P("gx", "gy", None, None),
        P("gx", "gy", None, None),
        P(),
        P(),
        P(),
        P(),
        P(),
        P(),
        P(),
    )
    out_specs = P("gx", "gy", None, None, None)
    return jax.shard_map(
        on_device, mesh=mesh, in_specs=in_specs, out_specs=out_specs, check_vma=False
    )
```

```python
import math

import jax
import jax.numpy as jnp
from jax import lax
from jax.sharding import PartitionSpec as P

NEIGHBOUR_SLOTS = 72
RBF = 16
ORBITAL_COUNT = 13
FILTER = 3


cutoff = 8.0
onsite_scale = 0.15

f32 = jnp.float32
bf16 = jnp.bfloat16


def shifted(value, axis, steps):
    count = lax.axis_size(axis)
    pairs = [(source, (source + steps) % count) for source in range(count)]
    return lax.ppermute(value, axis, pairs)


def bf16_parts(value):
    high = lax.reduce_precision(value, exponent_bits=8, mantissa_bits=7)
    rest = value - high
    middle = lax.reduce_precision(rest, exponent_bits=8, mantissa_bits=7)
    low = rest - middle
    return high.astype(bf16), middle.astype(bf16), low.astype(bf16)


def halo(flat):
    from_west = shifted(flat, "gx", 1)
    from_east = shifted(flat, "gx", -1)
    strip = jnp.stack([from_west, flat, from_east]).reshape(-1)
    from_south = shifted(strip, "gy", 1).reshape(3, -1)
    from_north = shifted(strip, "gy", -1).reshape(3, -1)
    strip = strip.reshape(3, -1)
    return jnp.stack([from_south, strip, from_north], axis=1).reshape(9, -1)


def first_halo(common, pairs):
    n = common.shape[0]
    m = pairs.shape[1]
    to_east = jnp.concatenate([common, pairs[6:9].reshape(-1)])
    to_west = jnp.concatenate([common, pairs[0:3].reshape(-1)])
    from_west = shifted(to_east, "gx", 1)
    from_east = shifted(to_west, "gx", -1)
    strip_common = jnp.stack([from_west[:n], common, from_east[:n]])
    strip_pairs = jnp.stack(
        [
            from_west[n:].reshape(3, m),
            pairs[3:6],
            from_east[n:].reshape(3, m),
        ]
    )
    to_north = jnp.concatenate([strip_common.reshape(-1), strip_pairs[:, 2].reshape(-1)])
    to_south = jnp.concatenate([strip_common.reshape(-1), strip_pairs[:, 0].reshape(-1)])
    from_south = shifted(to_north, "gy", 1)
    from_north = shifted(to_south, "gy", -1)
    all_common = jnp.stack(
        [from_south[: 3 * n].reshape(3, n), strip_common, from_north[: 3 * n].reshape(3, n)],
        axis=1,
    ).reshape(9, n)
    incoming = jnp.stack(
        [
            from_south[3 * n :].reshape(3, m),
            strip_pairs[:, 1],
            from_north[3 * n :].reshape(3, m),
        ],
        axis=1,
    ).reshape(9, m)
    return all_common, incoming


def pair_mixed(before_rows, distance, live_flags, radial_weight, mixing_weight, gate_weight):
    centres = cutoff * jnp.arange(RBF, dtype=f32) / (RBF - 1)
    spacing = cutoff / (RBF - 1)
    basis = jnp.exp(-jnp.square((distance[:, None] - centres[None, :]) / spacing)).astype(bf16)
    cutoff_envelope = jnp.square(1.0 - jnp.square(distance / cutoff))
    before = before_rows + jnp.dot(basis, radial_weight, preferred_element_type=f32)
    edge = jax.nn.silu(before).astype(bf16)
    opened = jax.nn.silu(jnp.dot(edge, mixing_weight, preferred_element_type=f32))
    mixed = (opened * jnp.dot(edge, gate_weight, preferred_element_type=f32)).astype(bf16)
    scale_factor = 1.5 / math.sqrt(NEIGHBOUR_SLOTS * ORBITAL_COUNT) * cutoff_envelope * live_flags
    return mixed, scale_factor


def on_device(
    features,
    atom_kinds,
    kind_table,
    band_vectors,
    pair_offsets,
    pair_source,
    pair_target,
    pair_live_mask,
    radial_weight,
    w_source,
    w_target,
    mixing_weight,
    gate_weight,
    output_weight,
    w_site,
):
    atom_count = features.shape[2]
    feat = features.shape[3]
    vec = band_vectors.shape[4]
    orb = ORBITAL_COUNT
    slots = pair_source.shape[3]
    kind_hot = (
        atom_kinds[0, 0][:, None] == jnp.arange(kind_table.shape[0], dtype=jnp.int32)[None, :]
    ).astype(f32)
    embedded = jnp.dot(kind_hot, kind_table, precision=lax.Precision.HIGHEST)
    atoms = (features[0, 0].astype(f32) + embedded).astype(bf16)

    offsets = pair_offsets[0, 0]
    distance = jnp.sqrt(offsets[0] * offsets[0] + offsets[1] * offsets[1] + offsets[2] * offsets[2])
    source = pair_source[0, 0]
    target = pair_target[0, 0]
    live = pair_live_mask[0, 0]
    high, middle, low = bf16_parts(distance)
    pair_data = jnp.stack(
        [source.astype(bf16), target.astype(bf16), live.astype(bf16), high, middle, low], axis=-1
    ).reshape(9, slots * 6)

    first = jnp.transpose(band_vectors[0, 0], (1, 0, 2))
    common = jnp.concatenate([atoms.reshape(-1), first.reshape(-1)])
    all_common, incoming = first_halo(common, pair_data)
    n_atoms = atom_count * feat
    ring_atoms = all_common[:, :n_atoms].reshape(9 * atom_count, feat)
    ring_first = all_common[:, n_atoms:]

    incoming = incoming.reshape(9, slots, 6).astype(f32)
    in_source = incoming[..., 0].astype(jnp.int32)
    in_target = incoming[..., 1].astype(jnp.int32)
    in_live = incoming[..., 2]
    in_distance = (incoming[..., 3] + incoming[..., 4]) + incoming[..., 5]

    places = jnp.arange(9, dtype=jnp.int32)[:, None] * atom_count
    centre = 4 * atom_count
    row_source = jnp.concatenate([(centre + source).reshape(-1), (places + in_source).reshape(-1)])
    row_target = jnp.concatenate([(places + target).reshape(-1), (centre + in_target).reshape(-1)])
    all_distance = jnp.concatenate([distance.reshape(-1), in_distance.reshape(-1)])
    all_live = jnp.concatenate([live.reshape(-1).astype(f32), in_live.reshape(-1)])

    source_projection = jnp.dot(ring_atoms, w_source, preferred_element_type=f32)
    target_projection = jnp.dot(ring_atoms, w_target, preferred_element_type=f32)
    table = jnp.concatenate([source_projection, target_projection])
    table_parts = jnp.concatenate(bf16_parts(table), axis=1)
    ring = 9 * atom_count
    columns = jnp.arange(2 * ring, dtype=jnp.int32)[None, :]
    pick = (
        (columns == row_source[:, None]) | (columns == (row_target[:, None] + ring))
    ).astype(bf16)
    picked = jnp.dot(pick, table_parts, preferred_element_type=f32)
    before_rows = (picked[:, :feat] + picked[:, feat : 2 * feat]) + picked[:, 2 * feat :]

    mixed, scale = pair_mixed(
        before_rows, all_distance, all_live, radial_weight, mixing_weight, gate_weight
    )
    weight_blocks = output_weight.reshape(feat, orb, orb)
    own_weight = jnp.swapaxes(weight_blocks, 1, 2).reshape(feat, orb * orb)
    own_raw = jnp.einsum("fb,sf->bs", own_weight, mixed[: 9 * slots], preferred_element_type=f32)
    in_raw = jnp.einsum("fb,sf->bs", output_weight, mixed[9 * slots :], preferred_element_type=f32)
    blocks_t = (jnp.concatenate([own_raw, in_raw], axis=1) * scale[None, :]).astype(bf16)

    square = jnp.dot(atoms, w_site, preferred_element_type=f32).reshape(-1, orb, orb)
    onsite = (onsite_scale * 0.5 * (square + jnp.swapaxes(square, 1, 2))).astype(bf16)
    onsite_t = jnp.transpose(onsite, (2, 1, 0)).reshape(orb * orb, atom_count)
    blocks_t = jnp.concatenate([blocks_t, onsite_t], axis=1)

    own_atoms = jnp.arange(atom_count, dtype=jnp.int32)
    row_atom = jnp.concatenate([source.reshape(-1), in_target.reshape(-1), own_atoms])
    column_atom = jnp.concatenate(
        [(places + target).reshape(-1), (places + in_source).reshape(-1), centre + own_atoms]
    )
    row_hot = (own_atoms[:, None] == row_atom[None, :]).astype(bf16)
    spread = (blocks_t[:, None, :] * row_hot[None, :, :]).reshape(orb * orb * atom_count, -1)
    column_hot = (column_atom[:, None] == jnp.arange(ring, dtype=jnp.int32)[None, :]).astype(bf16)
    dense = jnp.dot(spread, column_hot, preferred_element_type=f32).reshape(
        orb, orb * atom_count, ring
    )
    dense_parts = jnp.concatenate(bf16_parts(dense), axis=2)

    def apply(ring_vectors):
        by_orbital = jnp.swapaxes(ring_vectors.reshape(9, orb, atom_count, vec), 0, 1).reshape(
            orb, ring, vec
        )
        tripled = jnp.concatenate([by_orbital, by_orbital, by_orbital], axis=1)
        out = jnp.einsum("qak,qkv->qav", dense_parts, tripled, preferred_element_type=f32)
        return out.sum(axis=0).reshape(orb, atom_count, vec)

    previous = first.astype(f32)
    current = apply(ring_first)
    for repeat in range(FILTER - 1):
        ring_now = halo(current.astype(bf16).reshape(-1))
        upcoming = 2.0 * apply(ring_now) - previous
        previous, current = (current, upcoming)
    current = jnp.transpose(current, (1, 0, 2))
    return current[None, None]


def solution(mesh):
    in_specs = (
        P("gx", "gy", None, None),
        P("gx", "gy", None),
        P(),
        P("gx", "gy", None, None, None),
        P("gx", "gy", None, None, None),
        P("gx", "gy", None, None),
        P("gx", "gy", None, None),
        P("gx", "gy", None, None),
        P(),
        P(),
        P(),
        P(),
        P(),
        P(),
        P(),
    )
    out_specs = P("gx", "gy", None, None, None)
    return jax.shard_map(
        on_device, mesh=mesh, in_specs=in_specs, out_specs=out_specs, check_vma=False
    )
```

```python
import math

import jax
import jax.numpy as jnp
from jax import lax
from jax.sharding import PartitionSpec as P

NEIGHBOUR_SLOTS = 72
RBF = 16
ORBITAL_COUNT = 13
FILTER = 3


cutoff = 8.0
onsite_scale = 0.15

f32 = jnp.float32
bf16 = jnp.bfloat16


def shifted(value, axis, steps):
    count = lax.axis_size(axis)
    pairs = [(source, (source + steps) % count) for source in range(count)]
    return lax.ppermute(value, axis, pairs)


def bf16_parts(value):
    high = lax.reduce_precision(value, exponent_bits=8, mantissa_bits=7)
    rest = value - high
    middle = lax.reduce_precision(rest, exponent_bits=8, mantissa_bits=7)
    low = rest - middle
    return high.astype(bf16), middle.astype(bf16), low.astype(bf16)


def neighbour_shift(value, dx, dy):
    nx = lax.axis_size("gx")
    ny = lax.axis_size("gy")
    if dx == 0:
        return shifted(value, "gy", dy)
    if dy == 0:
        return shifted(value, "gx", dx)
    pairs = [
        (a * ny + b, ((a + dx) % nx) * ny + (b + dy) % ny) for a in range(nx) for b in range(ny)
    ]
    return lax.ppermute(value, ("gx", "gy"), pairs)


def halo(flat):
    places = []
    for u in range(9):
        if u == 4:
            places.append(flat)
        else:
            t = 8 - u
            places.append(neighbour_shift(flat, t // 3 - 1, t % 3 - 1))
    return jnp.stack(places)


def first_halo(common, pairs):
    n = common.shape[0]
    all_common = []
    incoming = []
    for u in range(9):
        t = 8 - u
        if u == 4:
            all_common.append(common)
            incoming.append(pairs[4])
        else:
            got = neighbour_shift(jnp.concatenate([common, pairs[t]]), t // 3 - 1, t % 3 - 1)
            all_common.append(got[:n])
            incoming.append(got[n:])
    return jnp.stack(all_common), jnp.stack(incoming)


def pair_mixed(before_rows, distance, live_flags, radial_weight, mixing_weight, gate_weight):
    centres = cutoff * jnp.arange(RBF, dtype=f32) / (RBF - 1)
    spacing = cutoff / (RBF - 1)
    basis = jnp.exp(-jnp.square((distance[:, None] - centres[None, :]) / spacing)).astype(bf16)
    cutoff_envelope = jnp.square(1.0 - jnp.square(distance / cutoff))
    before = before_rows + jnp.dot(basis, radial_weight, preferred_element_type=f32)
    edge = jax.nn.silu(before).astype(bf16)
    opened = jax.nn.silu(jnp.dot(edge, mixing_weight, preferred_element_type=f32))
    mixed = (opened * jnp.dot(edge, gate_weight, preferred_element_type=f32)).astype(bf16)
    scale_factor = 1.5 / math.sqrt(NEIGHBOUR_SLOTS * ORBITAL_COUNT) * cutoff_envelope * live_flags
    return mixed, scale_factor


def on_device(
    features,
    atom_kinds,
    kind_table,
    band_vectors,
    pair_offsets,
    pair_source,
    pair_target,
    pair_live_mask,
    radial_weight,
    w_source,
    w_target,
    mixing_weight,
    gate_weight,
    output_weight,
    w_site,
):
    atom_count = features.shape[2]
    feat = features.shape[3]
    vec = band_vectors.shape[4]
    orb = ORBITAL_COUNT
    slots = pair_source.shape[3]
    kind_hot = (
        atom_kinds[0, 0][:, None] == jnp.arange(kind_table.shape[0], dtype=jnp.int32)[None, :]
    ).astype(f32)
    embedded = jnp.dot(kind_hot, kind_table, precision=lax.Precision.HIGHEST)
    atoms = (features[0, 0].astype(f32) + embedded).astype(bf16)

    offsets = pair_offsets[0, 0]
    distance = jnp.sqrt(offsets[0] * offsets[0] + offsets[1] * offsets[1] + offsets[2] * offsets[2])
    source = pair_source[0, 0]
    target = pair_target[0, 0]
    live = pair_live_mask[0, 0]
    high, middle, low = bf16_parts(distance)
    pair_data = jnp.stack(
        [source.astype(bf16), target.astype(bf16), live.astype(bf16), high, middle, low], axis=-1
    ).reshape(9, slots * 6)

    first = jnp.transpose(band_vectors[0, 0], (1, 0, 2))
    common = jnp.concatenate([atoms.reshape(-1), first.reshape(-1)])
    all_common, incoming = first_halo(common, pair_data)
    n_atoms = atom_count * feat
    ring_atoms = all_common[:, :n_atoms].reshape(9 * atom_count, feat)
    ring_first = all_common[:, n_atoms:]

    incoming = incoming.reshape(9, slots, 6).astype(f32)
    in_source = incoming[..., 0].astype(jnp.int32)
    in_target = incoming[..., 1].astype(jnp.int32)
    in_live = incoming[..., 2]
    in_distance = (incoming[..., 3] + incoming[..., 4]) + incoming[..., 5]

    places = jnp.arange(9, dtype=jnp.int32)[:, None] * atom_count
    centre = 4 * atom_count
    row_source = jnp.concatenate([(centre + source).reshape(-1), (places + in_source).reshape(-1)])
    row_target = jnp.concatenate([(places + target).reshape(-1), (centre + in_target).reshape(-1)])
    all_distance = jnp.concatenate([distance.reshape(-1), in_distance.reshape(-1)])
    all_live = jnp.concatenate([live.reshape(-1).astype(f32), in_live.reshape(-1)])

    source_projection = jnp.dot(ring_atoms, w_source, preferred_element_type=f32)
    target_projection = jnp.dot(ring_atoms, w_target, preferred_element_type=f32)
    table = jnp.concatenate([source_projection, target_projection])
    table_parts = jnp.concatenate(bf16_parts(table), axis=1)
    ring = 9 * atom_count
    columns = jnp.arange(2 * ring, dtype=jnp.int32)[None, :]
    pick = (
        (columns == row_source[:, None]) | (columns == (row_target[:, None] + ring))
    ).astype(bf16)
    picked = jnp.dot(pick, table_parts, preferred_element_type=f32)
    before_rows = (picked[:, :feat] + picked[:, feat : 2 * feat]) + picked[:, 2 * feat :]

    mixed, scale = pair_mixed(
        before_rows, all_distance, all_live, radial_weight, mixing_weight, gate_weight
    )
    weight_blocks = output_weight.reshape(feat, orb, orb)
    own_weight = jnp.swapaxes(weight_blocks, 1, 2).reshape(feat, orb * orb)
    own_raw = jnp.einsum("fb,sf->bs", own_weight, mixed[: 9 * slots], preferred_element_type=f32)
    in_raw = jnp.einsum("fb,sf->bs", output_weight, mixed[9 * slots :], preferred_element_type=f32)
    blocks_t = (jnp.concatenate([own_raw, in_raw], axis=1) * scale[None, :]).astype(bf16)

    square = jnp.dot(atoms, w_site, preferred_element_type=f32).reshape(-1, orb, orb)
    onsite = (onsite_scale * 0.5 * (square + jnp.swapaxes(square, 1, 2))).astype(bf16)
    onsite_t = jnp.transpose(onsite, (2, 1, 0)).reshape(orb * orb, atom_count)
    blocks_t = jnp.concatenate([blocks_t, onsite_t], axis=1)

    own_atoms = jnp.arange(atom_count, dtype=jnp.int32)
    row_atom = jnp.concatenate([source.reshape(-1), in_target.reshape(-1), own_atoms])
    column_atom = jnp.concatenate(
        [(places + target).reshape(-1), (places + in_source).reshape(-1), centre + own_atoms]
    )
    row_hot = (own_atoms[:, None] == row_atom[None, :]).astype(bf16)
    spread = (blocks_t[:, None, :] * row_hot[None, :, :]).reshape(orb * orb * atom_count, -1)
    column_hot = (column_atom[:, None] == jnp.arange(ring, dtype=jnp.int32)[None, :]).astype(bf16)
    dense = jnp.dot(spread, column_hot, preferred_element_type=f32).reshape(
        orb, orb * atom_count, ring
    )
    dense_parts = jnp.concatenate(bf16_parts(dense), axis=2)

    def apply(ring_vectors):
        by_orbital = jnp.swapaxes(ring_vectors.reshape(9, orb, atom_count, vec), 0, 1).reshape(
            orb, ring, vec
        )
        tripled = jnp.concatenate([by_orbital, by_orbital, by_orbital], axis=1)
        out = jnp.einsum("qak,qkv->qav", dense_parts, tripled, preferred_element_type=f32)
        return out.sum(axis=0).reshape(orb, atom_count, vec)

    previous = first.astype(f32)
    current = apply(ring_first)
    for repeat in range(FILTER - 1):
        ring_now = halo(current.astype(bf16).reshape(-1))
        upcoming = 2.0 * apply(ring_now) - previous
        previous, current = (current, upcoming)
    current = jnp.transpose(current, (1, 0, 2))
    return current[None, None]


def solution(mesh):
    in_specs = (
        P("gx", "gy", None, None),
        P("gx", "gy", None),
        P(),
        P("gx", "gy", None, None, None),
        P("gx", "gy", None, None, None),
        P("gx", "gy", None, None),
        P("gx", "gy", None, None),
        P("gx", "gy", None, None),
        P(),
        P(),
        P(),
        P(),
        P(),
        P(),
        P(),
    )
    out_specs = P("gx", "gy", None, None, None)
    return jax.shard_map(
        on_device, mesh=mesh, in_specs=in_specs, out_specs=out_specs, check_vma=False
    )
```

```python
import math

import jax
import jax.numpy as jnp
from jax import lax
from jax.sharding import PartitionSpec as P

NEIGHBOUR_SLOTS = 72
RBF = 16
ORBITAL_COUNT = 13
FILTER = 3


cutoff = 8.0
onsite_scale = 0.15

f32 = jnp.float32
bf16 = jnp.bfloat16


def shifted(value, axis, steps):
    count = lax.axis_size(axis)
    pairs = [(source, (source + steps) % count) for source in range(count)]
    return lax.ppermute(value, axis, pairs)


def bf16_parts(value):
    high = lax.reduce_precision(value, exponent_bits=8, mantissa_bits=7)
    rest = value - high
    middle = lax.reduce_precision(rest, exponent_bits=8, mantissa_bits=7)
    low = rest - middle
    return high.astype(bf16), middle.astype(bf16), low.astype(bf16)


def halo(flat):
    from_west = shifted(flat, "gx", 1)
    from_east = shifted(flat, "gx", -1)
    strip = jnp.stack([from_west, flat, from_east]).reshape(-1)
    from_south = shifted(strip, "gy", 1).reshape(3, -1)
    from_north = shifted(strip, "gy", -1).reshape(3, -1)
    strip = strip.reshape(3, -1)
    return jnp.stack([from_south, strip, from_north], axis=1).reshape(9, -1)


def first_halo(common, pairs):
    n = common.shape[0]
    m = pairs.shape[1]
    to_east = jnp.concatenate([common, pairs[6:9].reshape(-1)])
    to_west = jnp.concatenate([common, pairs[0:3].reshape(-1)])
    from_west = shifted(to_east, "gx", 1)
    from_east = shifted(to_west, "gx", -1)
    strip_common = jnp.stack([from_west[:n], common, from_east[:n]])
    strip_pairs = jnp.stack(
        [
            from_west[n:].reshape(3, m),
            pairs[3:6],
            from_east[n:].reshape(3, m),
        ]
    )
    to_north = jnp.concatenate([strip_common.reshape(-1), strip_pairs[:, 2].reshape(-1)])
    to_south = jnp.concatenate([strip_common.reshape(-1), strip_pairs[:, 0].reshape(-1)])
    from_south = shifted(to_north, "gy", 1)
    from_north = shifted(to_south, "gy", -1)
    all_common = jnp.stack(
        [from_south[: 3 * n].reshape(3, n), strip_common, from_north[: 3 * n].reshape(3, n)],
        axis=1,
    ).reshape(9, n)
    incoming = jnp.stack(
        [
            from_south[3 * n :].reshape(3, m),
            strip_pairs[:, 1],
            from_north[3 * n :].reshape(3, m),
        ],
        axis=1,
    ).reshape(9, m)
    strip_incoming = strip_pairs[:, 1]
    return strip_common, strip_incoming, all_common, incoming


def pair_mixed(before_rows, distance, live_flags, radial_weight, mixing_weight, gate_weight):
    centres = cutoff * jnp.arange(RBF, dtype=f32) / (RBF - 1)
    spacing = cutoff / (RBF - 1)
    basis = jnp.exp(-jnp.square((distance[:, None] - centres[None, :]) / spacing)).astype(bf16)
    cutoff_envelope = jnp.square(1.0 - jnp.square(distance / cutoff))
    before = before_rows + jnp.dot(basis, radial_weight, preferred_element_type=f32)
    edge = jax.nn.silu(before).astype(bf16)
    opened = jax.nn.silu(jnp.dot(edge, mixing_weight, preferred_element_type=f32))
    mixed = (opened * jnp.dot(edge, gate_weight, preferred_element_type=f32)).astype(bf16)
    scale_factor = 1.5 / math.sqrt(NEIGHBOUR_SLOTS * ORBITAL_COUNT) * cutoff_envelope * live_flags
    return mixed, scale_factor


def on_device(
    features,
    atom_kinds,
    kind_table,
    band_vectors,
    pair_offsets,
    pair_source,
    pair_target,
    pair_live_mask,
    radial_weight,
    w_source,
    w_target,
    mixing_weight,
    gate_weight,
    output_weight,
    w_site,
):
    atom_count = features.shape[2]
    feat = features.shape[3]
    vec = band_vectors.shape[4]
    orb = ORBITAL_COUNT
    slots = pair_source.shape[3]
    kind_hot = (
        atom_kinds[0, 0][:, None] == jnp.arange(kind_table.shape[0], dtype=jnp.int32)[None, :]
    ).astype(f32)
    embedded = jnp.dot(kind_hot, kind_table, precision=lax.Precision.HIGHEST)
    atoms = (features[0, 0].astype(f32) + embedded).astype(bf16)

    offsets = pair_offsets[0, 0]
    distance = jnp.sqrt(offsets[0] * offsets[0] + offsets[1] * offsets[1] + offsets[2] * offsets[2])
    source = pair_source[0, 0]
    target = pair_target[0, 0]
    live = pair_live_mask[0, 0]
    high, middle, low = bf16_parts(distance)
    fields = 6
    pair_data = jnp.stack(
        [source.astype(bf16), target.astype(bf16), live.astype(bf16), high, middle, low], axis=1
    ).reshape(9, fields * slots)

    first = jnp.transpose(band_vectors[0, 0], (1, 0, 2))
    common = jnp.concatenate([atoms.reshape(-1), first.reshape(-1)])
    strip_common, strip_incoming, all_common, incoming = first_halo(common, pair_data)
    n_atoms = atom_count * feat
    ring_atoms = all_common[:, :n_atoms].reshape(9 * atom_count, feat)
    ring_first = all_common[:, n_atoms:]
    strip_atoms = strip_common[:, :n_atoms].reshape(3 * atom_count, feat)

    def unpack(received):
        received = received.reshape(-1, fields, slots).astype(f32)
        got_source = received[:, 0].astype(jnp.int32)
        got_target = received[:, 1].astype(jnp.int32)
        got_distance = (received[:, 3] + received[:, 4]) + received[:, 5]
        return got_source, got_target, received[:, 2], got_distance

    ring = 9 * atom_count
    weight_blocks = output_weight.reshape(feat, orb, orb)
    own_weight = jnp.swapaxes(weight_blocks, 1, 2).reshape(feat, orb * orb)
    own_atoms = jnp.arange(atom_count, dtype=jnp.int32)

    def group_dense(table_atoms, own_sets, in_source, in_target, in_distance, in_live, in_places, extra):
        width = table_atoms.shape[0]
        if width == ring:
            block_of = {u: u for u in range(9)}
        else:
            block_of = {1: 0, 4: 1, 7: 2}
        own_block = jnp.array([block_of[t] for t in own_sets], jnp.int32)[:, None] * atom_count
        in_block = jnp.array([block_of[u] for u in in_places], jnp.int32)[:, None] * atom_count
        centre_block = block_of[4] * atom_count
        own_ring = jnp.array(own_sets, jnp.int32)[:, None] * atom_count
        in_ring = jnp.array(in_places, jnp.int32)[:, None] * atom_count
        own_source = source[jnp.array(own_sets)]
        own_target = target[jnp.array(own_sets)]
        row_source = jnp.concatenate(
            [(centre_block + own_source).reshape(-1), (in_block + in_source).reshape(-1)]
        )
        row_target = jnp.concatenate(
            [(own_block + own_target).reshape(-1), (centre_block + in_target).reshape(-1)]
        )
        group_distance = jnp.concatenate(
            [distance[jnp.array(own_sets)].reshape(-1), in_distance.reshape(-1)]
        )
        group_live = jnp.concatenate(
            [live[jnp.array(own_sets)].reshape(-1).astype(f32), in_live.reshape(-1)]
        )
        source_projection = jnp.dot(table_atoms, w_source, preferred_element_type=f32)
        target_projection = jnp.dot(table_atoms, w_target, preferred_element_type=f32)
        table = jnp.concatenate([source_projection, target_projection])
        table_parts = jnp.concatenate(bf16_parts(table), axis=1)
        columns = jnp.arange(2 * width, dtype=jnp.int32)[None, :]
        pick = (
            (columns == row_source[:, None]) | (columns == (row_target[:, None] + width))
        ).astype(bf16)
        picked = jnp.dot(pick, table_parts, preferred_element_type=f32)
        before_rows = (picked[:, :feat] + picked[:, feat : 2 * feat]) + picked[:, 2 * feat :]
        mixed, scale = pair_mixed(
            before_rows, group_distance, group_live, radial_weight, mixing_weight, gate_weight
        )
        own_count = len(own_sets) * slots
        own_raw = jnp.einsum("fb,sf->bs", own_weight, mixed[:own_count], preferred_element_type=f32)
        in_raw = jnp.einsum("fb,sf->bs", output_weight, mixed[own_count:], preferred_element_type=f32)
        blocks_t = (jnp.concatenate([own_raw, in_raw], axis=1) * scale[None, :]).astype(bf16)
        row_atom = jnp.concatenate([own_source.reshape(-1), in_target.reshape(-1)])
        column_atom = jnp.concatenate(
            [(own_ring + own_target).reshape(-1), (in_ring + in_source).reshape(-1)]
        )
        if extra is not None:
            blocks_t = jnp.concatenate([blocks_t, extra], axis=1)
            row_atom = jnp.concatenate([row_atom, own_atoms])
            column_atom = jnp.concatenate([column_atom, 4 * atom_count + own_atoms])
        row_hot = (own_atoms[:, None] == row_atom[None, :]).astype(bf16)
        spread = (blocks_t[:, None, :] * row_hot[None, :, :]).reshape(orb * orb * atom_count, -1)
        column_hot = (column_atom[:, None] == jnp.arange(ring, dtype=jnp.int32)[None, :]).astype(bf16)
        return jnp.dot(spread, column_hot, preferred_element_type=f32)

    square = jnp.dot(atoms, w_site, preferred_element_type=f32).reshape(-1, orb, orb)
    onsite = (onsite_scale * 0.5 * (square + jnp.swapaxes(square, 1, 2))).astype(bf16)
    onsite_t = jnp.transpose(onsite, (2, 1, 0)).reshape(orb * orb, atom_count)

    strip_places = (1, 4, 7)
    s_source, s_target, s_live, s_distance = unpack(strip_incoming)
    dense = group_dense(
        strip_atoms, strip_places, s_source, s_target, s_distance, s_live, strip_places, onsite_t
    )
    rest_places = (0, 2, 3, 5, 6, 8)
    r_source, r_target, r_live, r_distance = unpack(incoming[jnp.array(rest_places)])
    dense = dense + group_dense(
        ring_atoms, rest_places, r_source, r_target, r_distance, r_live, rest_places, None
    )
    dense = dense.reshape(orb, orb * atom_count, ring)
    dense_parts = jnp.concatenate(bf16_parts(dense), axis=2)

    def apply(ring_vectors):
        by_orbital = jnp.swapaxes(ring_vectors.reshape(9, orb, atom_count, vec), 0, 1).reshape(
            orb, ring, vec
        )
        tripled = jnp.concatenate([by_orbital, by_orbital, by_orbital], axis=1)
        out = jnp.einsum("qak,qkv->qav", dense_parts, tripled, preferred_element_type=f32)
        return out.sum(axis=0).reshape(orb, atom_count, vec)

    previous = first.astype(f32)
    current = apply(ring_first)
    for repeat in range(FILTER - 1):
        ring_now = halo(current.astype(bf16).reshape(-1))
        upcoming = 2.0 * apply(ring_now) - previous
        previous, current = (current, upcoming)
    current = jnp.transpose(current, (1, 0, 2))
    return current[None, None]


def solution(mesh):
    in_specs = (
        P("gx", "gy", None, None),
        P("gx", "gy", None),
        P(),
        P("gx", "gy", None, None, None),
        P("gx", "gy", None, None, None),
        P("gx", "gy", None, None),
        P("gx", "gy", None, None),
        P("gx", "gy", None, None),
        P(),
        P(),
        P(),
        P(),
        P(),
        P(),
        P(),
    )
    out_specs = P("gx", "gy", None, None, None)
    return jax.shard_map(
        on_device, mesh=mesh, in_specs=in_specs, out_specs=out_specs, check_vma=False
    )
```

```python
import math

import jax
import jax.numpy as jnp
from jax import lax
from jax.sharding import PartitionSpec as P

NEIGHBOUR_SLOTS = 72
RBF = 16
ORBITAL_COUNT = 13
FILTER = 3


cutoff = 8.0
onsite_scale = 0.15

f32 = jnp.float32
bf16 = jnp.bfloat16


def shifted(value, axis, steps):
    count = lax.axis_size(axis)
    pairs = [(source, (source + steps) % count) for source in range(count)]
    return lax.ppermute(value, axis, pairs)


def bf16_parts(value):
    high = lax.reduce_precision(value, exponent_bits=8, mantissa_bits=7)
    rest = value - high
    middle = lax.reduce_precision(rest, exponent_bits=8, mantissa_bits=7)
    low = rest - middle
    return high.astype(bf16), middle.astype(bf16), low.astype(bf16)


def halo(flat):
    from_west = shifted(flat, "gx", 1)
    from_east = shifted(flat, "gx", -1)
    strip = jnp.stack([from_west, flat, from_east]).reshape(-1)
    from_south = shifted(strip, "gy", 1).reshape(3, -1)
    from_north = shifted(strip, "gy", -1).reshape(3, -1)
    strip = strip.reshape(3, -1)
    return jnp.stack([from_south, strip, from_north], axis=1).reshape(9, -1)


def first_halo(common, pairs):
    n = common.shape[0]
    m = pairs.shape[1]
    to_east = jnp.concatenate([common, pairs[6:9].reshape(-1)])
    to_west = jnp.concatenate([common, pairs[0:3].reshape(-1)])
    from_west = shifted(to_east, "gx", 1)
    from_east = shifted(to_west, "gx", -1)
    strip_common = jnp.stack([from_west[:n], common, from_east[:n]])
    strip_pairs = jnp.stack(
        [
            from_west[n:].reshape(3, m),
            pairs[3:6],
            from_east[n:].reshape(3, m),
        ]
    )
    to_north = jnp.concatenate([strip_common.reshape(-1), strip_pairs[:, 2].reshape(-1)])
    to_south = jnp.concatenate([strip_common.reshape(-1), strip_pairs[:, 0].reshape(-1)])
    from_south = shifted(to_north, "gy", 1)
    from_north = shifted(to_south, "gy", -1)
    all_common = jnp.stack(
        [from_south[: 3 * n].reshape(3, n), strip_common, from_north[: 3 * n].reshape(3, n)],
        axis=1,
    ).reshape(9, n)
    incoming = jnp.stack(
        [
            from_south[3 * n :].reshape(3, m),
            strip_pairs[:, 1],
            from_north[3 * n :].reshape(3, m),
        ],
        axis=1,
    ).reshape(9, m)
    return all_common, incoming


def pair_mixed(before_rows, distance, live_flags, radial_weight, mixing_weight, gate_weight):
    centres = cutoff * jnp.arange(RBF, dtype=f32) / (RBF - 1)
    spacing = cutoff / (RBF - 1)
    basis = jnp.exp(-jnp.square((distance[:, None] - centres[None, :]) / spacing)).astype(bf16)
    cutoff_envelope = jnp.square(1.0 - jnp.square(distance / cutoff))
    before = before_rows + jnp.dot(basis, radial_weight, preferred_element_type=f32)
    edge = jax.nn.silu(before).astype(bf16)
    opened = jax.nn.silu(jnp.dot(edge, mixing_weight, preferred_element_type=f32))
    mixed = (opened * jnp.dot(edge, gate_weight, preferred_element_type=f32)).astype(bf16)
    scale_factor = 1.5 / math.sqrt(NEIGHBOUR_SLOTS * ORBITAL_COUNT) * cutoff_envelope * live_flags
    return mixed, scale_factor


def on_device(
    features,
    atom_kinds,
    kind_table,
    band_vectors,
    pair_offsets,
    pair_source,
    pair_target,
    pair_live_mask,
    radial_weight,
    w_source,
    w_target,
    mixing_weight,
    gate_weight,
    output_weight,
    w_site,
):
    atom_count = features.shape[2]
    feat = features.shape[3]
    vec = band_vectors.shape[4]
    orb = ORBITAL_COUNT
    slots = pair_source.shape[3]
    kind_hot = (
        atom_kinds[0, 0][:, None] == jnp.arange(kind_table.shape[0], dtype=jnp.int32)[None, :]
    ).astype(f32)
    embedded = jnp.dot(kind_hot, kind_table, precision=lax.Precision.HIGHEST)
    atoms = (features[0, 0].astype(f32) + embedded).astype(bf16)

    offsets = pair_offsets[0, 0]
    distance = jnp.sqrt(offsets[0] * offsets[0] + offsets[1] * offsets[1] + offsets[2] * offsets[2])
    source = pair_source[0, 0]
    target = pair_target[0, 0]
    live = pair_live_mask[0, 0]
    high, middle, low = bf16_parts(distance)
    pair_data = jnp.stack(
        [source.astype(bf16), target.astype(bf16), live.astype(bf16), high, middle, low], axis=1
    ).reshape(9, 6 * slots)

    common = jnp.concatenate([atoms.reshape(-1), band_vectors[0, 0].reshape(-1)])
    all_common, incoming = first_halo(common, pair_data)
    n_atoms = atom_count * feat
    ring_atoms = all_common[:, :n_atoms].reshape(9 * atom_count, feat)
    ring_first = all_common[:, n_atoms:]

    incoming = incoming.reshape(9, 6, slots).astype(f32)
    in_source = incoming[:, 0].astype(jnp.int32)
    in_target = incoming[:, 1].astype(jnp.int32)
    in_live = incoming[:, 2]
    in_distance = (incoming[:, 3] + incoming[:, 4]) + incoming[:, 5]

    places = jnp.arange(9, dtype=jnp.int32)[:, None] * atom_count
    centre = 4 * atom_count
    row_source = jnp.concatenate([(centre + source).reshape(-1), (places + in_source).reshape(-1)])
    row_target = jnp.concatenate([(places + target).reshape(-1), (centre + in_target).reshape(-1)])
    all_distance = jnp.concatenate([distance.reshape(-1), in_distance.reshape(-1)])
    all_live = jnp.concatenate([live.reshape(-1).astype(f32), in_live.reshape(-1)])

    source_projection = jnp.dot(ring_atoms, w_source, preferred_element_type=f32)
    target_projection = jnp.dot(ring_atoms, w_target, preferred_element_type=f32)
    table = jnp.concatenate([source_projection, target_projection])
    table_parts = jnp.concatenate(bf16_parts(table), axis=1)
    ring = 9 * atom_count
    columns = jnp.arange(2 * ring, dtype=jnp.int32)[None, :]
    pick = (
        (columns == row_source[:, None]) | (columns == (row_target[:, None] + ring))
    ).astype(bf16)
    picked = jnp.dot(pick, table_parts, preferred_element_type=f32)
    before_rows = (picked[:, :feat] + picked[:, feat : 2 * feat]) + picked[:, 2 * feat :]

    mixed, scale = pair_mixed(
        before_rows, all_distance, all_live, radial_weight, mixing_weight, gate_weight
    )
    weight_blocks = output_weight.reshape(feat, orb, orb)
    own_weight = jnp.swapaxes(weight_blocks, 1, 2).reshape(feat, orb * orb)
    own_raw = jnp.einsum("fb,sf->bs", own_weight, mixed[: 9 * slots], preferred_element_type=f32)
    in_raw = jnp.einsum("fb,sf->bs", output_weight, mixed[9 * slots :], preferred_element_type=f32)
    blocks_t = (jnp.concatenate([own_raw, in_raw], axis=1) * scale[None, :]).astype(bf16)

    square = jnp.dot(atoms, w_site, preferred_element_type=f32).reshape(-1, orb, orb)
    onsite = (onsite_scale * 0.5 * (square + jnp.swapaxes(square, 1, 2))).astype(bf16)
    onsite_t = jnp.transpose(onsite, (2, 1, 0)).reshape(orb * orb, atom_count)
    blocks_t = jnp.concatenate([blocks_t, onsite_t], axis=1)

    own_atoms = jnp.arange(atom_count, dtype=jnp.int32)
    row_atom = jnp.concatenate([source.reshape(-1), in_target.reshape(-1), own_atoms])
    column_atom = jnp.concatenate(
        [(places + target).reshape(-1), (places + in_source).reshape(-1), centre + own_atoms]
    )
    row_hot = (own_atoms[:, None] == row_atom[None, :]).astype(bf16)
    spread = (blocks_t[:, None, :] * row_hot[None, :, :]).reshape(orb * orb * atom_count, -1)
    column_hot = (column_atom[:, None] == jnp.arange(ring, dtype=jnp.int32)[None, :]).astype(bf16)
    dense = jnp.dot(spread, column_hot, preferred_element_type=f32).reshape(
        orb, orb * atom_count, ring
    )
    dense_high, dense_middle, _ = bf16_parts(dense)
    dense_parts = jnp.concatenate([dense_high, dense_middle], axis=2)

    def apply(ring_vectors):
        by_orbital = jnp.swapaxes(ring_vectors.reshape(9, orb, atom_count, vec), 0, 1).reshape(
            orb, ring, vec
        )
        doubled = jnp.concatenate([by_orbital, by_orbital], axis=1)
        out = jnp.einsum("qak,qkv->qav", dense_parts, doubled, preferred_element_type=f32)
        return out.sum(axis=0).reshape(orb, atom_count, vec)

    first = jnp.transpose(band_vectors[0, 0], (1, 0, 2))
    previous = first.astype(f32)
    ring_first = jnp.transpose(
        ring_first.reshape(9, atom_count, orb, vec), (0, 2, 1, 3)
    ).reshape(9, -1)
    current = apply(ring_first)
    for repeat in range(FILTER - 1):
        ring_now = halo(current.astype(bf16).reshape(-1))
        upcoming = 2.0 * apply(ring_now) - previous
        previous, current = (current, upcoming)
    current = jnp.transpose(current, (1, 0, 2))
    return current[None, None]


def solution(mesh):
    in_specs = (
        P("gx", "gy", None, None),
        P("gx", "gy", None),
        P(),
        P("gx", "gy", None, None, None),
        P("gx", "gy", None, None, None),
        P("gx", "gy", None, None),
        P("gx", "gy", None, None),
        P("gx", "gy", None, None),
        P(),
        P(),
        P(),
        P(),
        P(),
        P(),
        P(),
    )
    out_specs = P("gx", "gy", None, None, None)
    return jax.shard_map(
        on_device, mesh=mesh, in_specs=in_specs, out_specs=out_specs, check_vma=False
    )
```

```python
import math

import jax
import jax.numpy as jnp
from jax import lax
from jax.sharding import PartitionSpec as P

NEIGHBOUR_SLOTS = 72
RBF = 16
ORBITAL_COUNT = 13
FILTER = 3


cutoff = 8.0
onsite_scale = 0.15

f32 = jnp.float32
bf16 = jnp.bfloat16


def shifted(value, axis, steps):
    count = lax.axis_size(axis)
    pairs = [(source, (source + steps) % count) for source in range(count)]
    return lax.ppermute(value, axis, pairs)


def bf16_parts(value):
    high = lax.reduce_precision(value, exponent_bits=8, mantissa_bits=7)
    rest = value - high
    middle = lax.reduce_precision(rest, exponent_bits=8, mantissa_bits=7)
    low = rest - middle
    return high.astype(bf16), middle.astype(bf16), low.astype(bf16)


def halo(flat):
    from_west = shifted(flat, "gx", 1)
    from_east = shifted(flat, "gx", -1)
    strip = jnp.stack([from_west, flat, from_east]).reshape(-1)
    from_south = shifted(strip, "gy", 1).reshape(3, -1)
    from_north = shifted(strip, "gy", -1).reshape(3, -1)
    strip = strip.reshape(3, -1)
    return jnp.stack([from_south, strip, from_north], axis=1).reshape(9, -1)


def first_halo(common, pairs):
    n = common.shape[0]
    m = pairs.shape[1]
    to_east = jnp.concatenate([common, pairs[6:9].reshape(-1)])
    to_west = jnp.concatenate([common, pairs[0:3].reshape(-1)])
    from_west = shifted(to_east, "gx", 1)
    from_east = shifted(to_west, "gx", -1)
    strip_common = jnp.stack([from_west[:n], common, from_east[:n]])
    strip_pairs = jnp.stack(
        [
            from_west[n:].reshape(3, m),
            pairs[3:6],
            from_east[n:].reshape(3, m),
        ]
    )
    to_north = jnp.concatenate([strip_common.reshape(-1), strip_pairs[:, 2].reshape(-1)])
    to_south = jnp.concatenate([strip_common.reshape(-1), strip_pairs[:, 0].reshape(-1)])
    from_south = shifted(to_north, "gy", 1)
    from_north = shifted(to_south, "gy", -1)
    all_common = jnp.stack(
        [from_south[: 3 * n].reshape(3, n), strip_common, from_north[: 3 * n].reshape(3, n)],
        axis=1,
    ).reshape(9, n)
    incoming = jnp.stack(
        [
            from_south[3 * n :].reshape(3, m),
            strip_pairs[:, 1],
            from_north[3 * n :].reshape(3, m),
        ],
        axis=1,
    ).reshape(9, m)
    return strip_common, strip_pairs[:, 1], all_common, incoming


def pair_mixed(before_rows, distance, live_flags, radial_weight, mixing_weight, gate_weight):
    centres = cutoff * jnp.arange(RBF, dtype=f32) / (RBF - 1)
    spacing = cutoff / (RBF - 1)
    basis = jnp.exp(-jnp.square((distance[:, None] - centres[None, :]) / spacing)).astype(bf16)
    cutoff_envelope = jnp.square(1.0 - jnp.square(distance / cutoff))
    before = before_rows + jnp.dot(basis, radial_weight, preferred_element_type=f32)
    edge = jax.nn.silu(before).astype(bf16)
    opened = jax.nn.silu(jnp.dot(edge, mixing_weight, preferred_element_type=f32))
    mixed = (opened * jnp.dot(edge, gate_weight, preferred_element_type=f32)).astype(bf16)
    scale_factor = 1.5 / math.sqrt(NEIGHBOUR_SLOTS * ORBITAL_COUNT) * cutoff_envelope * live_flags
    return mixed, scale_factor


def on_device(
    features,
    atom_kinds,
    kind_table,
    band_vectors,
    pair_offsets,
    pair_source,
    pair_target,
    pair_live_mask,
    radial_weight,
    w_source,
    w_target,
    mixing_weight,
    gate_weight,
    output_weight,
    w_site,
):
    atom_count = features.shape[2]
    feat = features.shape[3]
    vec = band_vectors.shape[4]
    orb = ORBITAL_COUNT
    slots = pair_source.shape[3]
    kind_hot = (
        atom_kinds[0, 0][:, None] == jnp.arange(kind_table.shape[0], dtype=jnp.int32)[None, :]
    ).astype(f32)
    embedded = jnp.dot(kind_hot, kind_table, precision=lax.Precision.HIGHEST)
    atoms = (features[0, 0].astype(f32) + embedded).astype(bf16)

    offsets = pair_offsets[0, 0]
    distance = jnp.sqrt(offsets[0] * offsets[0] + offsets[1] * offsets[1] + offsets[2] * offsets[2])
    source = pair_source[0, 0]
    target = pair_target[0, 0]
    live = pair_live_mask[0, 0]
    high, middle, low = bf16_parts(distance)
    pair_data = jnp.stack(
        [source.astype(bf16), target.astype(bf16), live.astype(bf16), high, middle, low], axis=1
    ).reshape(9, 6 * slots)

    common = jnp.concatenate([atoms.reshape(-1), band_vectors[0, 0].reshape(-1)])
    strip_common, strip_incoming, all_common, incoming = first_halo(common, pair_data)
    n_atoms = atom_count * feat
    ring_atoms = all_common[:, :n_atoms].reshape(9 * atom_count, feat)
    ring_first = all_common[:, n_atoms:]
    strip_atoms = strip_common[:, :n_atoms].reshape(3 * atom_count, feat)

    def unpack(received):
        received = received.reshape(-1, 6, slots).astype(f32)
        got_distance = (received[:, 3] + received[:, 4]) + received[:, 5]
        return (
            received[:, 0].astype(jnp.int32),
            received[:, 1].astype(jnp.int32),
            received[:, 2],
            got_distance,
        )

    def rest(values):
        return jnp.concatenate([values[0::3], values[2::3]])

    ring = 9 * atom_count
    weight_blocks = output_weight.reshape(feat, orb, orb)
    own_weight = jnp.swapaxes(weight_blocks, 1, 2).reshape(feat, orb * orb)

    def group_blocks(table_atoms, own_index, in_index, own_sets, in_sets):
        own_source, own_target, own_live, own_distance = own_sets
        in_source, in_target, in_live, in_distance = in_sets
        width = table_atoms.shape[0]
        centre_index = atom_count * (width // (2 * atom_count))
        row_source = jnp.concatenate(
            [(centre_index + own_source).reshape(-1), (in_index + in_source).reshape(-1)]
        )
        row_target = jnp.concatenate(
            [(own_index + own_target).reshape(-1), (centre_index + in_target).reshape(-1)]
        )
        group_distance = jnp.concatenate([own_distance.reshape(-1), in_distance.reshape(-1)])
        group_live = jnp.concatenate([own_live.reshape(-1), in_live.reshape(-1)])
        source_projection = jnp.dot(table_atoms, w_source, preferred_element_type=f32)
        target_projection = jnp.dot(table_atoms, w_target, preferred_element_type=f32)
        table = jnp.concatenate([source_projection, target_projection])
        table_parts = jnp.concatenate(bf16_parts(table), axis=1)
        columns = jnp.arange(2 * width, dtype=jnp.int32)[None, :]
        pick = (
            (columns == row_source[:, None]) | (columns == (row_target[:, None] + width))
        ).astype(bf16)
        picked = jnp.dot(pick, table_parts, preferred_element_type=f32)
        before_rows = (picked[:, :feat] + picked[:, feat : 2 * feat]) + picked[:, 2 * feat :]
        mixed, scale = pair_mixed(
            before_rows, group_distance, group_live, radial_weight, mixing_weight, gate_weight
        )
        own_count = own_source.size
        own_raw = jnp.einsum("fb,sf->bs", own_weight, mixed[:own_count], preferred_element_type=f32)
        in_raw = jnp.einsum("fb,sf->bs", output_weight, mixed[own_count:], preferred_element_type=f32)
        return (jnp.concatenate([own_raw, in_raw], axis=1) * scale[None, :]).astype(bf16)

    live_f = live.astype(f32)
    strip_sets = (source[1::3], target[1::3], live_f[1::3], distance[1::3])
    strip_in = unpack(strip_incoming)
    three = jnp.arange(3, dtype=jnp.int32)[:, None] * atom_count
    strip_blocks = group_blocks(strip_atoms, three, three, strip_sets, strip_in)

    rest_sets = (rest(source), rest(target), rest(live_f), rest(distance))
    rest_in = unpack(rest(incoming))
    rest_places = rest(jnp.arange(9, dtype=jnp.int32))[:, None] * atom_count
    rest_blocks = group_blocks(ring_atoms, rest_places, rest_places, rest_sets, rest_in)

    square = jnp.dot(atoms, w_site, preferred_element_type=f32).reshape(-1, orb, orb)
    onsite = (onsite_scale * 0.5 * (square + jnp.swapaxes(square, 1, 2))).astype(bf16)
    onsite_t = jnp.transpose(onsite, (2, 1, 0)).reshape(orb * orb, atom_count)
    blocks_t = jnp.concatenate([strip_blocks, rest_blocks, onsite_t], axis=1)

    own_atoms = jnp.arange(atom_count, dtype=jnp.int32)
    strip_places = jnp.array([1, 4, 7], jnp.int32)[:, None] * atom_count
    centre = 4 * atom_count
    row_atom = jnp.concatenate(
        [
            strip_sets[0].reshape(-1),
            strip_in[1].reshape(-1),
            rest_sets[0].reshape(-1),
            rest_in[1].reshape(-1),
            own_atoms,
        ]
    )
    column_atom = jnp.concatenate(
        [
            (strip_places + strip_sets[1]).reshape(-1),
            (strip_places + strip_in[0]).reshape(-1),
            (rest_places + rest_sets[1]).reshape(-1),
            (rest_places + rest_in[0]).reshape(-1),
            centre + own_atoms,
        ]
    )
    row_hot = (own_atoms[:, None] == row_atom[None, :]).astype(bf16)
    spread = (blocks_t[:, None, :] * row_hot[None, :, :]).reshape(orb * orb * atom_count, -1)
    column_hot = (column_atom[:, None] == jnp.arange(ring, dtype=jnp.int32)[None, :]).astype(bf16)
    dense = jnp.dot(spread, column_hot, preferred_element_type=f32).reshape(
        orb, orb * atom_count, ring
    )
    dense_high, dense_middle, _ = bf16_parts(dense)
    dense_parts = jnp.concatenate([dense_high, dense_middle], axis=2)

    def apply(ring_vectors):
        by_orbital = jnp.swapaxes(ring_vectors.reshape(9, orb, atom_count, vec), 0, 1).reshape(
            orb, ring, vec
        )
        doubled = jnp.concatenate([by_orbital, by_orbital], axis=1)
        out = jnp.einsum("qak,qkv->qav", dense_parts, doubled, preferred_element_type=f32)
        return out.sum(axis=0).reshape(orb, atom_count, vec)

    first = jnp.transpose(band_vectors[0, 0], (1, 0, 2))
    previous = first.astype(f32)
    ring_first = jnp.transpose(
        ring_first.reshape(9, atom_count, orb, vec), (0, 2, 1, 3)
    ).reshape(9, -1)
    current = apply(ring_first)
    for repeat in range(FILTER - 1):
        ring_now = halo(current.astype(bf16).reshape(-1))
        upcoming = 2.0 * apply(ring_now) - previous
        previous, current = (current, upcoming)
    current = jnp.transpose(current, (1, 0, 2))
    return current[None, None]


def solution(mesh):
    in_specs = (
        P("gx", "gy", None, None),
        P("gx", "gy", None),
        P(),
        P("gx", "gy", None, None, None),
        P("gx", "gy", None, None, None),
        P("gx", "gy", None, None),
        P("gx", "gy", None, None),
        P("gx", "gy", None, None),
        P(),
        P(),
        P(),
        P(),
        P(),
        P(),
        P(),
    )
    out_specs = P("gx", "gy", None, None, None)
    return jax.shard_map(
        on_device, mesh=mesh, in_specs=in_specs, out_specs=out_specs, check_vma=False
    )
```

```python
import math

import jax
import jax.numpy as jnp
from jax import lax
from jax.sharding import PartitionSpec as P

NEIGHBOUR_SLOTS = 72
RBF = 16
ORBITAL_COUNT = 13
FILTER = 3


cutoff = 8.0
onsite_scale = 0.15

f32 = jnp.float32
bf16 = jnp.bfloat16


def shifted(value, axis, steps):
    count = lax.axis_size(axis)
    pairs = [(source, (source + steps) % count) for source in range(count)]
    return lax.ppermute(value, axis, pairs)


def bf16_parts(value):
    high = lax.reduce_precision(value, exponent_bits=8, mantissa_bits=7)
    rest = value - high
    middle = lax.reduce_precision(rest, exponent_bits=8, mantissa_bits=7)
    low = rest - middle
    return high.astype(bf16), middle.astype(bf16), low.astype(bf16)


def halo(flat):
    from_west = shifted(flat, "gx", 1)
    from_east = shifted(flat, "gx", -1)
    strip = jnp.stack([from_west, flat, from_east]).reshape(-1)
    from_south = shifted(strip, "gy", 1).reshape(3, -1)
    from_north = shifted(strip, "gy", -1).reshape(3, -1)
    strip = strip.reshape(3, -1)
    return jnp.stack([from_south, strip, from_north], axis=1).reshape(9, -1)


def first_halo(common, pairs):
    n = common.shape[0]
    m = pairs.shape[1]
    to_east = jnp.concatenate([common, pairs[6:9].reshape(-1)])
    to_west = jnp.concatenate([common, pairs[0:3].reshape(-1)])
    from_west = shifted(to_east, "gx", 1)
    from_east = shifted(to_west, "gx", -1)
    strip_common = jnp.stack([from_west[:n], common, from_east[:n]])
    strip_pairs = jnp.stack(
        [
            from_west[n:].reshape(3, m),
            pairs[3:6],
            from_east[n:].reshape(3, m),
        ]
    )
    to_north = jnp.concatenate([strip_common.reshape(-1), strip_pairs[:, 2].reshape(-1)])
    to_south = jnp.concatenate([strip_common.reshape(-1), strip_pairs[:, 0].reshape(-1)])
    from_south = shifted(to_north, "gy", 1)
    from_north = shifted(to_south, "gy", -1)
    all_common = jnp.stack(
        [from_south[: 3 * n].reshape(3, n), strip_common, from_north[: 3 * n].reshape(3, n)],
        axis=1,
    ).reshape(9, n)
    incoming = jnp.stack(
        [
            from_south[3 * n :].reshape(3, m),
            strip_pairs[:, 1],
            from_north[3 * n :].reshape(3, m),
        ],
        axis=1,
    ).reshape(9, m)
    return strip_common, strip_pairs[:, 1], all_common, incoming


def pair_mixed(before_rows, distance, live_flags, radial_weight, mixing_weight, gate_weight):
    centres = cutoff * jnp.arange(RBF, dtype=f32) / (RBF - 1)
    spacing = cutoff / (RBF - 1)
    basis = jnp.exp(-jnp.square((distance[:, None] - centres[None, :]) / spacing)).astype(bf16)
    cutoff_envelope = jnp.square(1.0 - jnp.square(distance / cutoff))
    before = before_rows + jnp.dot(basis, radial_weight, preferred_element_type=f32)
    edge = jax.nn.silu(before).astype(bf16)
    opened = jax.nn.silu(jnp.dot(edge, mixing_weight, preferred_element_type=f32))
    mixed = (opened * jnp.dot(edge, gate_weight, preferred_element_type=f32)).astype(bf16)
    scale_factor = 1.5 / math.sqrt(NEIGHBOUR_SLOTS * ORBITAL_COUNT) * cutoff_envelope * live_flags
    return mixed, scale_factor


def on_device(
    features,
    atom_kinds,
    kind_table,
    band_vectors,
    pair_offsets,
    pair_source,
    pair_target,
    pair_live_mask,
    radial_weight,
    w_source,
    w_target,
    mixing_weight,
    gate_weight,
    output_weight,
    w_site,
):
    atom_count = features.shape[2]
    feat = features.shape[3]
    vec = band_vectors.shape[4]
    orb = ORBITAL_COUNT
    slots = pair_source.shape[3]
    kind_hot = (
        atom_kinds[0, 0][:, None] == jnp.arange(kind_table.shape[0], dtype=jnp.int32)[None, :]
    ).astype(f32)
    embedded = jnp.dot(kind_hot, kind_table, precision=lax.Precision.HIGHEST)
    atoms = (features[0, 0].astype(f32) + embedded).astype(bf16)

    offsets = pair_offsets[0, 0]
    distance = jnp.sqrt(offsets[0] * offsets[0] + offsets[1] * offsets[1] + offsets[2] * offsets[2])
    source = pair_source[0, 0]
    target = pair_target[0, 0]
    live = pair_live_mask[0, 0]
    high = lax.reduce_precision(distance, exponent_bits=8, mantissa_bits=7)
    rest_distance = distance - high
    middle = lax.reduce_precision(rest_distance, exponent_bits=8, mantissa_bits=7)
    low = rest_distance - middle
    field = lax.broadcasted_iota(jnp.int32, (9, 6, slots), 1)
    fields = [source.astype(f32), target.astype(f32), live.astype(f32), high, middle, low]
    pair_data = fields[5][:, None, :]
    for index in range(4, -1, -1):
        pair_data = jnp.where(field == index, fields[index][:, None, :], pair_data)
    pair_data = pair_data.astype(bf16).reshape(9, 6 * slots)

    common = jnp.concatenate([atoms.reshape(-1), band_vectors[0, 0].reshape(-1)])
    strip_common, strip_incoming, all_common, incoming = first_halo(common, pair_data)
    n_atoms = atom_count * feat
    ring_atoms = all_common[:, :n_atoms].reshape(9 * atom_count, feat)
    ring_first = all_common[:, n_atoms:]
    strip_atoms = strip_common[:, :n_atoms].reshape(3 * atom_count, feat)

    def unpack(received):
        received = received.reshape(-1, 6, slots).astype(f32)
        got_distance = (received[:, 3] + received[:, 4]) + received[:, 5]
        return (
            received[:, 0].astype(jnp.int32),
            received[:, 1].astype(jnp.int32),
            received[:, 2],
            got_distance,
        )

    def rest(values):
        return jnp.concatenate([values[0::3], values[2::3]])

    ring = 9 * atom_count
    weight_blocks = output_weight.reshape(feat, orb, orb)
    own_weight = jnp.swapaxes(weight_blocks, 1, 2).reshape(feat, orb * orb)

    def group_blocks(table_atoms, own_index, in_index, own_sets, in_sets):
        own_source, own_target, own_live, own_distance = own_sets
        in_source, in_target, in_live, in_distance = in_sets
        width = table_atoms.shape[0]
        centre_index = atom_count * (width // (2 * atom_count))
        row_source = jnp.concatenate(
            [(centre_index + own_source).reshape(-1), (in_index + in_source).reshape(-1)]
        )
        row_target = jnp.concatenate(
            [(own_index + own_target).reshape(-1), (centre_index + in_target).reshape(-1)]
        )
        group_distance = jnp.concatenate([own_distance.reshape(-1), in_distance.reshape(-1)])
        group_live = jnp.concatenate([own_live.reshape(-1), in_live.reshape(-1)])
        source_projection = jnp.dot(table_atoms, w_source, preferred_element_type=f32)
        target_projection = jnp.dot(table_atoms, w_target, preferred_element_type=f32)
        table = jnp.concatenate([source_projection, target_projection])
        table_parts = jnp.concatenate(bf16_parts(table), axis=1)
        columns = jnp.arange(2 * width, dtype=jnp.int32)[None, :]
        pick = (
            (columns == row_source[:, None]) | (columns == (row_target[:, None] + width))
        ).astype(bf16)
        picked = jnp.dot(pick, table_parts, preferred_element_type=f32)
        before_rows = (picked[:, :feat] + picked[:, feat : 2 * feat]) + picked[:, 2 * feat :]
        mixed, scale = pair_mixed(
            before_rows, group_distance, group_live, radial_weight, mixing_weight, gate_weight
        )
        own_count = own_source.size
        own_raw = jnp.einsum("fb,sf->bs", own_weight, mixed[:own_count], preferred_element_type=f32)
        in_raw = jnp.einsum("fb,sf->bs", output_weight, mixed[own_count:], preferred_element_type=f32)
        return (jnp.concatenate([own_raw, in_raw], axis=1) * scale[None, :]).astype(bf16)

    live_f = live.astype(f32)
    strip_sets = (source[1::3], target[1::3], live_f[1::3], distance[1::3])
    strip_in = unpack(strip_incoming)
    three = jnp.arange(3, dtype=jnp.int32)[:, None] * atom_count
    strip_blocks = group_blocks(strip_atoms, three, three, strip_sets, strip_in)

    rest_sets = (rest(source), rest(target), rest(live_f), rest(distance))
    rest_in = unpack(rest(incoming))
    rest_places = rest(jnp.arange(9, dtype=jnp.int32))[:, None] * atom_count
    rest_blocks = group_blocks(ring_atoms, rest_places, rest_places, rest_sets, rest_in)

    square = jnp.dot(atoms, w_site, preferred_element_type=f32).reshape(-1, orb, orb)
    onsite = (onsite_scale * 0.5 * (square + jnp.swapaxes(square, 1, 2))).astype(bf16)
    onsite_t = jnp.transpose(onsite, (2, 1, 0)).reshape(orb * orb, atom_count)
    blocks_t = jnp.concatenate([strip_blocks, rest_blocks, onsite_t], axis=1)

    own_atoms = jnp.arange(atom_count, dtype=jnp.int32)
    strip_places = jnp.array([1, 4, 7], jnp.int32)[:, None] * atom_count
    centre = 4 * atom_count
    row_atom = jnp.concatenate(
        [
            strip_sets[0].reshape(-1),
            strip_in[1].reshape(-1),
            rest_sets[0].reshape(-1),
            rest_in[1].reshape(-1),
            own_atoms,
        ]
    )
    column_atom = jnp.concatenate(
        [
            (strip_places + strip_sets[1]).reshape(-1),
            (strip_places + strip_in[0]).reshape(-1),
            (rest_places + rest_sets[1]).reshape(-1),
            (rest_places + rest_in[0]).reshape(-1),
            centre + own_atoms,
        ]
    )
    row_hot = (own_atoms[:, None] == row_atom[None, :]).astype(bf16)
    spread = (blocks_t[:, None, :] * row_hot[None, :, :]).reshape(orb * orb * atom_count, -1)
    column_hot = (column_atom[:, None] == jnp.arange(ring, dtype=jnp.int32)[None, :]).astype(bf16)
    dense = jnp.dot(spread, column_hot, preferred_element_type=f32).reshape(
        orb, orb * atom_count, ring
    )
    dense_high, dense_middle, _ = bf16_parts(dense)
    dense_parts = jnp.concatenate([dense_high, dense_middle], axis=2)

    def apply(ring_vectors):
        by_orbital = jnp.swapaxes(ring_vectors.reshape(9, orb, atom_count, vec), 0, 1).reshape(
            orb, ring, vec
        )
        doubled = jnp.concatenate([by_orbital, by_orbital], axis=1)
        out = jnp.einsum("qak,qkv->qav", dense_parts, doubled, preferred_element_type=f32)
        return out.sum(axis=0).reshape(orb, atom_count, vec)

    first = jnp.transpose(band_vectors[0, 0], (1, 0, 2))
    previous = first.astype(f32)
    ring_first = jnp.transpose(
        ring_first.reshape(9, atom_count, orb, vec), (0, 2, 1, 3)
    ).reshape(9, -1)
    current = apply(ring_first)
    for repeat in range(FILTER - 1):
        ring_now = halo(current.astype(bf16).reshape(-1))
        upcoming = 2.0 * apply(ring_now) - previous
        previous, current = (current, upcoming)
    current = jnp.transpose(current, (1, 0, 2))
    return current[None, None]


def solution(mesh):
    in_specs = (
        P("gx", "gy", None, None),
        P("gx", "gy", None),
        P(),
        P("gx", "gy", None, None, None),
        P("gx", "gy", None, None, None),
        P("gx", "gy", None, None),
        P("gx", "gy", None, None),
        P("gx", "gy", None, None),
        P(),
        P(),
        P(),
        P(),
        P(),
        P(),
        P(),
    )
    out_specs = P("gx", "gy", None, None, None)
    return jax.shard_map(
        on_device, mesh=mesh, in_specs=in_specs, out_specs=out_specs, check_vma=False
    )
```

```python
import math

import jax
import jax.numpy as jnp
from jax import lax
from jax.sharding import PartitionSpec as P

NEIGHBOUR_SLOTS = 72
RBF = 16
ORBITAL_COUNT = 13
FILTER = 3


cutoff = 8.0
onsite_scale = 0.15

f32 = jnp.float32
bf16 = jnp.bfloat16


def shifted(value, axis, steps):
    count = lax.axis_size(axis)
    pairs = [(source, (source + steps) % count) for source in range(count)]
    return lax.ppermute(value, axis, pairs)


def bf16_parts(value):
    high = lax.reduce_precision(value, exponent_bits=8, mantissa_bits=7)
    rest = value - high
    middle = lax.reduce_precision(rest, exponent_bits=8, mantissa_bits=7)
    low = rest - middle
    return high.astype(bf16), middle.astype(bf16), low.astype(bf16)


def gy_swaps(to_south, to_north):
    count = lax.axis_size("gy")
    even = lax.axis_index("gy") % 2 == 0
    on_chip = lax.ppermute(
        jnp.where(even, to_north, to_south), "gy", [(i, i ^ 1) for i in range(count)]
    )
    across = lax.ppermute(
        jnp.where(even, to_south, to_north),
        "gy",
        [(i, (i + 1) % count if i % 2 else (i - 1) % count) for i in range(count)],
    )
    return jnp.where(even, across, on_chip), jnp.where(even, on_chip, across)


def halo(flat):
    from_west = shifted(flat, "gx", 1)
    from_east = shifted(flat, "gx", -1)
    strip = jnp.stack([from_west, flat, from_east]).reshape(-1)
    from_south, from_north = gy_swaps(strip, strip)
    from_south = from_south.reshape(3, -1)
    from_north = from_north.reshape(3, -1)
    strip = strip.reshape(3, -1)
    return jnp.stack([from_south, strip, from_north], axis=1).reshape(9, -1)


def first_halo(common, pairs):
    n = common.shape[0]
    m = pairs.shape[1]
    to_east = jnp.concatenate([common, pairs[6:9].reshape(-1)])
    to_west = jnp.concatenate([common, pairs[0:3].reshape(-1)])
    from_west = shifted(to_east, "gx", 1)
    from_east = shifted(to_west, "gx", -1)
    strip_common = jnp.stack([from_west[:n], common, from_east[:n]])
    strip_pairs = jnp.stack(
        [
            from_west[n:].reshape(3, m),
            pairs[3:6],
            from_east[n:].reshape(3, m),
        ]
    )
    to_north = jnp.concatenate([strip_common.reshape(-1), strip_pairs[:, 2].reshape(-1)])
    to_south = jnp.concatenate([strip_common.reshape(-1), strip_pairs[:, 0].reshape(-1)])
    from_south, from_north = gy_swaps(to_south, to_north)
    all_common = jnp.stack(
        [from_south[: 3 * n].reshape(3, n), strip_common, from_north[: 3 * n].reshape(3, n)],
        axis=1,
    ).reshape(9, n)
    incoming = jnp.stack(
        [
            from_south[3 * n :].reshape(3, m),
            strip_pairs[:, 1],
            from_north[3 * n :].reshape(3, m),
        ],
        axis=1,
    ).reshape(9, m)
    return strip_common, strip_pairs[:, 1], all_common, incoming


def pair_mixed(before_rows, distance, live_flags, radial_weight, mixing_weight, gate_weight):
    centres = cutoff * jnp.arange(RBF, dtype=f32) / (RBF - 1)
    spacing = cutoff / (RBF - 1)
    basis = jnp.exp(-jnp.square((distance[:, None] - centres[None, :]) / spacing)).astype(bf16)
    cutoff_envelope = jnp.square(1.0 - jnp.square(distance / cutoff))
    before = before_rows + jnp.dot(basis, radial_weight, preferred_element_type=f32)
    edge = jax.nn.silu(before).astype(bf16)
    opened = jax.nn.silu(jnp.dot(edge, mixing_weight, preferred_element_type=f32))
    mixed = (opened * jnp.dot(edge, gate_weight, preferred_element_type=f32)).astype(bf16)
    scale_factor = 1.5 / math.sqrt(NEIGHBOUR_SLOTS * ORBITAL_COUNT) * cutoff_envelope * live_flags
    return mixed, scale_factor


def on_device(
    features,
    atom_kinds,
    kind_table,
    band_vectors,
    pair_offsets,
    pair_source,
    pair_target,
    pair_live_mask,
    radial_weight,
    w_source,
    w_target,
    mixing_weight,
    gate_weight,
    output_weight,
    w_site,
):
    atom_count = features.shape[2]
    feat = features.shape[3]
    vec = band_vectors.shape[4]
    orb = ORBITAL_COUNT
    slots = pair_source.shape[3]
    kind_hot = (
        atom_kinds[0, 0][:, None] == jnp.arange(kind_table.shape[0], dtype=jnp.int32)[None, :]
    ).astype(f32)
    embedded = jnp.dot(kind_hot, kind_table, precision=lax.Precision.HIGHEST)
    atoms = (features[0, 0].astype(f32) + embedded).astype(bf16)

    offsets = pair_offsets[0, 0]
    distance = jnp.sqrt(offsets[0] * offsets[0] + offsets[1] * offsets[1] + offsets[2] * offsets[2])
    source = pair_source[0, 0]
    target = pair_target[0, 0]
    live = pair_live_mask[0, 0]
    high = lax.reduce_precision(distance, exponent_bits=8, mantissa_bits=7)
    rest_distance = distance - high
    middle = lax.reduce_precision(rest_distance, exponent_bits=8, mantissa_bits=7)
    low = rest_distance - middle
    field = lax.broadcasted_iota(jnp.int32, (9, 6, slots), 1)
    fields = [source.astype(f32), target.astype(f32), live.astype(f32), high, middle, low]
    pair_data = fields[5][:, None, :]
    for index in range(4, -1, -1):
        pair_data = jnp.where(field == index, fields[index][:, None, :], pair_data)
    pair_data = pair_data.astype(bf16).reshape(9, 6 * slots)

    common = jnp.concatenate([atoms.reshape(-1), band_vectors[0, 0].reshape(-1)])
    strip_common, strip_incoming, all_common, incoming = first_halo(common, pair_data)
    n_atoms = atom_count * feat
    ring_atoms = all_common[:, :n_atoms].reshape(9 * atom_count, feat)
    ring_first = all_common[:, n_atoms:]
    strip_atoms = strip_common[:, :n_atoms].reshape(3 * atom_count, feat)

    def unpack(received):
        received = received.reshape(-1, 6, slots).astype(f32)
        got_distance = (received[:, 3] + received[:, 4]) + received[:, 5]
        return (
            received[:, 0].astype(jnp.int32),
            received[:, 1].astype(jnp.int32),
            received[:, 2],
            got_distance,
        )

    def rest(values):
        return jnp.concatenate([values[0::3], values[2::3]])

    ring = 9 * atom_count
    weight_blocks = output_weight.reshape(feat, orb, orb)
    own_weight = jnp.swapaxes(weight_blocks, 1, 2).reshape(feat, orb * orb)

    def group_blocks(table_atoms, own_index, in_index, own_sets, in_sets):
        own_source, own_target, own_live, own_distance = own_sets
        in_source, in_target, in_live, in_distance = in_sets
        width = table_atoms.shape[0]
        centre_index = atom_count * (width // (2 * atom_count))
        row_source = jnp.concatenate(
            [(centre_index + own_source).reshape(-1), (in_index + in_source).reshape(-1)]
        )
        row_target = jnp.concatenate(
            [(own_index + own_target).reshape(-1), (centre_index + in_target).reshape(-1)]
        )
        group_distance = jnp.concatenate([own_distance.reshape(-1), in_distance.reshape(-1)])
        group_live = jnp.concatenate([own_live.reshape(-1), in_live.reshape(-1)])
        source_projection = jnp.dot(table_atoms, w_source, preferred_element_type=f32)
        target_projection = jnp.dot(table_atoms, w_target, preferred_element_type=f32)
        table = jnp.concatenate([source_projection, target_projection])
        table_parts = jnp.concatenate(bf16_parts(table), axis=1)
        columns = jnp.arange(2 * width, dtype=jnp.int32)[None, :]
        pick = (
            (columns == row_source[:, None]) | (columns == (row_target[:, None] + width))
        ).astype(bf16)
        picked = jnp.dot(pick, table_parts, preferred_element_type=f32)
        before_rows = (picked[:, :feat] + picked[:, feat : 2 * feat]) + picked[:, 2 * feat :]
        mixed, scale = pair_mixed(
            before_rows, group_distance, group_live, radial_weight, mixing_weight, gate_weight
        )
        own_count = own_source.size
        own_raw = jnp.einsum("fb,sf->bs", own_weight, mixed[:own_count], preferred_element_type=f32)
        in_raw = jnp.einsum("fb,sf->bs", output_weight, mixed[own_count:], preferred_element_type=f32)
        return (jnp.concatenate([own_raw, in_raw], axis=1) * scale[None, :]).astype(bf16)

    live_f = live.astype(f32)
    strip_sets = (source[1::3], target[1::3], live_f[1::3], distance[1::3])
    strip_in = unpack(strip_incoming)
    three = jnp.arange(3, dtype=jnp.int32)[:, None] * atom_count
    strip_blocks = group_blocks(strip_atoms, three, three, strip_sets, strip_in)

    rest_sets = (rest(source), rest(target), rest(live_f), rest(distance))
    rest_in = unpack(rest(incoming))
    rest_places = rest(jnp.arange(9, dtype=jnp.int32))[:, None] * atom_count
    rest_blocks = group_blocks(ring_atoms, rest_places, rest_places, rest_sets, rest_in)

    square = jnp.dot(atoms, w_site, preferred_element_type=f32).reshape(-1, orb, orb)
    onsite = (onsite_scale * 0.5 * (square + jnp.swapaxes(square, 1, 2))).astype(bf16)
    onsite_t = jnp.transpose(onsite, (2, 1, 0)).reshape(orb * orb, atom_count)
    blocks_t = jnp.concatenate([strip_blocks, rest_blocks, onsite_t], axis=1)

    own_atoms = jnp.arange(atom_count, dtype=jnp.int32)
    strip_places = jnp.array([1, 4, 7], jnp.int32)[:, None] * atom_count
    centre = 4 * atom_count
    row_atom = jnp.concatenate(
        [
            strip_sets[0].reshape(-1),
            strip_in[1].reshape(-1),
            rest_sets[0].reshape(-1),
            rest_in[1].reshape(-1),
            own_atoms,
        ]
    )
    column_atom = jnp.concatenate(
        [
            (strip_places + strip_sets[1]).reshape(-1),
            (strip_places + strip_in[0]).reshape(-1),
            (rest_places + rest_sets[1]).reshape(-1),
            (rest_places + rest_in[0]).reshape(-1),
            centre + own_atoms,
        ]
    )
    row_hot = (own_atoms[:, None] == row_atom[None, :]).astype(bf16)
    spread = (blocks_t[:, None, :] * row_hot[None, :, :]).reshape(orb * orb * atom_count, -1)
    column_hot = (column_atom[:, None] == jnp.arange(ring, dtype=jnp.int32)[None, :]).astype(bf16)
    dense = jnp.dot(spread, column_hot, preferred_element_type=f32).reshape(
        orb, orb * atom_count, ring
    )
    dense_high, dense_middle, _ = bf16_parts(dense)
    dense_parts = jnp.concatenate([dense_high, dense_middle], axis=2)

    def apply(ring_vectors):
        by_orbital = jnp.swapaxes(ring_vectors.reshape(9, orb, atom_count, vec), 0, 1).reshape(
            orb, ring, vec
        )
        doubled = jnp.concatenate([by_orbital, by_orbital], axis=1)
        out = jnp.einsum("qak,qkv->qav", dense_parts, doubled, preferred_element_type=f32)
        return out.sum(axis=0).reshape(orb, atom_count, vec)

    first = jnp.transpose(band_vectors[0, 0], (1, 0, 2))
    previous = first.astype(f32)
    ring_first = jnp.transpose(
        ring_first.reshape(9, atom_count, orb, vec), (0, 2, 1, 3)
    ).reshape(9, -1)
    current = apply(ring_first)
    for repeat in range(FILTER - 1):
        ring_now = halo(current.astype(bf16).reshape(-1))
        upcoming = 2.0 * apply(ring_now) - previous
        previous, current = (current, upcoming)
    current = jnp.transpose(current, (1, 0, 2))
    return current[None, None]


def solution(mesh):
    in_specs = (
        P("gx", "gy", None, None),
        P("gx", "gy", None),
        P(),
        P("gx", "gy", None, None, None),
        P("gx", "gy", None, None, None),
        P("gx", "gy", None, None),
        P("gx", "gy", None, None),
        P("gx", "gy", None, None),
        P(),
        P(),
        P(),
        P(),
        P(),
        P(),
        P(),
    )
    out_specs = P("gx", "gy", None, None, None)
    return jax.shard_map(
        on_device, mesh=mesh, in_specs=in_specs, out_specs=out_specs, check_vma=False
    )
```

```python
import math

import jax
import jax.numpy as jnp
from jax import lax
from jax.sharding import PartitionSpec as P

NEIGHBOUR_SLOTS = 72
RBF = 16
ORBITAL_COUNT = 13
FILTER = 3


cutoff = 8.0
onsite_scale = 0.15

f32 = jnp.float32
bf16 = jnp.bfloat16


def shifted(value, axis, steps):
    count = lax.axis_size(axis)
    pairs = [(source, (source + steps) % count) for source in range(count)]
    return lax.ppermute(value, axis, pairs)


def bf16_parts(value):
    high = lax.reduce_precision(value, exponent_bits=8, mantissa_bits=7)
    rest = value - high
    middle = lax.reduce_precision(rest, exponent_bits=8, mantissa_bits=7)
    low = rest - middle
    return high.astype(bf16), middle.astype(bf16), low.astype(bf16)


def halo(flat):
    from_west = shifted(flat, "gx", 1)
    from_east = shifted(flat, "gx", -1)
    strip = jnp.stack([from_west, flat, from_east]).reshape(-1)
    from_south = shifted(strip, "gy", 1).reshape(3, -1)
    from_north = shifted(strip, "gy", -1).reshape(3, -1)
    strip = strip.reshape(3, -1)
    return jnp.stack([from_south, strip, from_north], axis=1).reshape(9, -1)


def first_halo(common, pairs):
    n = common.shape[0]
    m = pairs.shape[1]
    to_east = jnp.concatenate([common, pairs[6:9].reshape(-1)])
    to_west = jnp.concatenate([common, pairs[0:3].reshape(-1)])
    from_west = shifted(to_east, "gx", 1)
    from_east = shifted(to_west, "gx", -1)
    strip_common = jnp.stack([from_west[:n], common, from_east[:n]])
    strip_pairs = jnp.stack(
        [
            from_west[n:].reshape(3, m),
            pairs[3:6],
            from_east[n:].reshape(3, m),
        ]
    )
    to_north = jnp.concatenate([strip_common.reshape(-1), strip_pairs[:, 2].reshape(-1)])
    to_south = jnp.concatenate([strip_common.reshape(-1), strip_pairs[:, 0].reshape(-1)])
    from_south = shifted(to_north, "gy", 1)
    from_north = shifted(to_south, "gy", -1)
    all_common = jnp.stack(
        [from_south[: 3 * n].reshape(3, n), strip_common, from_north[: 3 * n].reshape(3, n)],
        axis=1,
    ).reshape(9, n)
    incoming = jnp.stack(
        [
            from_south[3 * n :].reshape(3, m),
            strip_pairs[:, 1],
            from_north[3 * n :].reshape(3, m),
        ],
        axis=1,
    ).reshape(9, m)
    return strip_common, strip_pairs[:, 1], all_common, incoming


def pair_mixed(before_rows, distance, live_flags, radial_weight, mixing_weight, gate_weight):
    centres = cutoff * jnp.arange(RBF, dtype=f32) / (RBF - 1)
    spacing = cutoff / (RBF - 1)
    basis = jnp.exp(-jnp.square((distance[:, None] - centres[None, :]) / spacing)).astype(bf16)
    cutoff_envelope = jnp.square(1.0 - jnp.square(distance / cutoff))
    before = before_rows + jnp.dot(basis, radial_weight, preferred_element_type=f32)
    edge = jax.nn.silu(before).astype(bf16)
    opened = jax.nn.silu(jnp.dot(edge, mixing_weight, preferred_element_type=f32))
    mixed = (opened * jnp.dot(edge, gate_weight, preferred_element_type=f32)).astype(bf16)
    scale_factor = 1.5 / math.sqrt(NEIGHBOUR_SLOTS * ORBITAL_COUNT) * cutoff_envelope * live_flags
    return mixed, scale_factor


def on_device(
    features,
    atom_kinds,
    kind_table,
    band_vectors,
    pair_offsets,
    pair_source,
    pair_target,
    pair_live_mask,
    radial_weight,
    w_source,
    w_target,
    mixing_weight,
    gate_weight,
    output_weight,
    w_site,
):
    atom_count = features.shape[2]
    feat = features.shape[3]
    vec = band_vectors.shape[4]
    orb = ORBITAL_COUNT
    slots = pair_source.shape[3]
    kind_hot = (
        atom_kinds[0, 0][:, None] == jnp.arange(kind_table.shape[0], dtype=jnp.int32)[None, :]
    ).astype(f32)
    embedded = jnp.dot(kind_hot, kind_table, precision=lax.Precision.HIGHEST)
    atoms = (features[0, 0].astype(f32) + embedded).astype(bf16)

    offsets = pair_offsets[0, 0]
    distance = jnp.sqrt(offsets[0] * offsets[0] + offsets[1] * offsets[1] + offsets[2] * offsets[2])
    source = pair_source[0, 0]
    target = pair_target[0, 0]
    live = pair_live_mask[0, 0]
    high, middle, low = bf16_parts(distance)
    pair_data = jnp.stack(
        [source.astype(bf16), target.astype(bf16), live.astype(bf16), high, middle, low], axis=1
    ).reshape(9, 6 * slots)

    common = jnp.concatenate([atoms.reshape(-1), band_vectors[0, 0].reshape(-1)])
    strip_common, strip_incoming, all_common, incoming = first_halo(common, pair_data)
    n_atoms = atom_count * feat
    ring_atoms = all_common[:, :n_atoms].reshape(9 * atom_count, feat)
    ring_first = all_common[:, n_atoms:]
    strip_atoms = strip_common[:, :n_atoms].reshape(3 * atom_count, feat)

    def unpack(received):
        received = received.reshape(-1, 6, slots).astype(f32)
        got_distance = (received[:, 3] + received[:, 4]) + received[:, 5]
        return (
            received[:, 0].astype(jnp.int32),
            received[:, 1].astype(jnp.int32),
            received[:, 2],
            got_distance,
        )

    def rest(values):
        return jnp.concatenate([values[0::3], values[2::3]])

    ring = 9 * atom_count
    weight_blocks = output_weight.reshape(feat, orb, orb)
    own_weight = jnp.swapaxes(weight_blocks, 1, 2).reshape(feat, orb * orb)

    def group_blocks(table_atoms, own_index, in_index, own_sets, in_sets):
        own_source, own_target, own_live, own_distance = own_sets
        in_source, in_target, in_live, in_distance = in_sets
        width = table_atoms.shape[0]
        centre_index = atom_count * (width // (2 * atom_count))
        row_source = jnp.concatenate(
            [(centre_index + own_source).reshape(-1), (in_index + in_source).reshape(-1)]
        )
        row_target = jnp.concatenate(
            [(own_index + own_target).reshape(-1), (centre_index + in_target).reshape(-1)]
        )
        group_distance = jnp.concatenate([own_distance.reshape(-1), in_distance.reshape(-1)])
        group_live = jnp.concatenate([own_live.reshape(-1), in_live.reshape(-1)])
        source_projection = jnp.dot(table_atoms, w_source, preferred_element_type=f32)
        target_projection = jnp.dot(table_atoms, w_target, preferred_element_type=f32)
        table = jnp.concatenate([source_projection, target_projection])
        table_parts = jnp.concatenate(bf16_parts(table), axis=1)
        columns = jnp.arange(2 * width, dtype=jnp.int32)[None, :]
        pick = (
            (columns == row_source[:, None]) | (columns == (row_target[:, None] + width))
        ).astype(bf16)
        picked = jnp.dot(pick, table_parts, preferred_element_type=f32)
        before_rows = (picked[:, :feat] + picked[:, feat : 2 * feat]) + picked[:, 2 * feat :]
        mixed, scale = pair_mixed(
            before_rows, group_distance, group_live, radial_weight, mixing_weight, gate_weight
        )
        own_count = own_source.size
        own_raw = jnp.einsum("fb,sf->bs", own_weight, mixed[:own_count], preferred_element_type=f32)
        in_raw = jnp.einsum("fb,sf->bs", output_weight, mixed[own_count:], preferred_element_type=f32)
        return (jnp.concatenate([own_raw, in_raw], axis=1) * scale[None, :]).astype(bf16)

    live_f = live.astype(f32)
    strip_sets = (source[1::3], target[1::3], live_f[1::3], distance[1::3])
    strip_in = unpack(strip_incoming)
    three = jnp.arange(3, dtype=jnp.int32)[:, None] * atom_count
    strip_blocks = group_blocks(strip_atoms, three, three, strip_sets, strip_in)

    rest_sets = (rest(source), rest(target), rest(live_f), rest(distance))
    rest_in = unpack(rest(incoming))
    rest_places = rest(jnp.arange(9, dtype=jnp.int32))[:, None] * atom_count
    rest_blocks = group_blocks(ring_atoms, rest_places, rest_places, rest_sets, rest_in)

    square = jnp.dot(atoms, w_site, preferred_element_type=f32).reshape(-1, orb, orb)
    onsite = (onsite_scale * 0.5 * (square + jnp.swapaxes(square, 1, 2))).astype(bf16)
    onsite_t = jnp.transpose(onsite, (2, 1, 0)).reshape(orb * orb, atom_count)
    blocks_t = jnp.concatenate([strip_blocks, rest_blocks, onsite_t], axis=1)

    own_atoms = jnp.arange(atom_count, dtype=jnp.int32)
    strip_places = jnp.array([1, 4, 7], jnp.int32)[:, None] * atom_count
    centre = 4 * atom_count
    row_atom = jnp.concatenate(
        [
            strip_sets[0].reshape(-1),
            strip_in[1].reshape(-1),
            rest_sets[0].reshape(-1),
            rest_in[1].reshape(-1),
            own_atoms,
        ]
    )
    column_atom = jnp.concatenate(
        [
            (strip_places + strip_sets[1]).reshape(-1),
            (strip_places + strip_in[0]).reshape(-1),
            (rest_places + rest_sets[1]).reshape(-1),
            (rest_places + rest_in[0]).reshape(-1),
            centre + own_atoms,
        ]
    )
    row_hot = (own_atoms[:, None] == row_atom[None, :]).astype(bf16)
    spread = (blocks_t[:, None, :] * row_hot[None, :, :]).reshape(orb * orb * atom_count, -1)
    column_hot = (column_atom[:, None] == jnp.arange(ring, dtype=jnp.int32)[None, :]).astype(bf16)
    dense = jnp.dot(spread, column_hot, preferred_element_type=f32).reshape(
        orb, orb * atom_count, ring
    )
    dense_high, dense_middle, _ = bf16_parts(dense)
    dense_parts = jnp.concatenate([dense_high, dense_middle], axis=2)

    def apply(ring_vectors):
        by_orbital = jnp.swapaxes(ring_vectors.reshape(9, orb, atom_count, vec), 0, 1).reshape(
            orb, ring, vec
        )
        doubled = jnp.concatenate([by_orbital, by_orbital], axis=1)
        out = jnp.einsum("qak,qkv->qav", dense_parts, doubled, preferred_element_type=f32)
        return out.sum(axis=0).reshape(orb, atom_count, vec)

    def first_apply(ring_vectors):
        by_orbital = jnp.swapaxes(ring_vectors.reshape(9, orb, atom_count, vec), 0, 1).reshape(
            orb, ring, vec
        )
        gathered = jnp.einsum("qcv,sc->qvs", by_orbital, column_hot, preferred_element_type=f32)
        blocks3 = blocks_t.reshape(orb, orb, -1).astype(f32)
        products = jnp.sum(blocks3[:, :, None, :] * gathered[:, None, :, :], axis=0)
        parts = jnp.concatenate(bf16_parts(products), axis=0)
        out = jnp.einsum("pvs,rs->prv", parts, row_hot, preferred_element_type=f32)
        return out.reshape(3, orb, atom_count, vec).sum(axis=0)

    first = jnp.transpose(band_vectors[0, 0], (1, 0, 2))
    previous = first.astype(f32)
    ring_first = jnp.transpose(
        ring_first.reshape(9, atom_count, orb, vec), (0, 2, 1, 3)
    ).reshape(9, -1)
    current = first_apply(ring_first)
    for repeat in range(FILTER - 1):
        ring_now = halo(current.astype(bf16).reshape(-1))
        upcoming = 2.0 * apply(ring_now) - previous
        previous, current = (current, upcoming)
    current = jnp.transpose(current, (1, 0, 2))
    return current[None, None]


def solution(mesh):
    in_specs = (
        P("gx", "gy", None, None),
        P("gx", "gy", None),
        P(),
        P("gx", "gy", None, None, None),
        P("gx", "gy", None, None, None),
        P("gx", "gy", None, None),
        P("gx", "gy", None, None),
        P("gx", "gy", None, None),
        P(),
        P(),
        P(),
        P(),
        P(),
        P(),
        P(),
    )
    out_specs = P("gx", "gy", None, None, None)
    return jax.shard_map(
        on_device, mesh=mesh, in_specs=in_specs, out_specs=out_specs, check_vma=False
    )
```

```python
import math

import jax
import jax.numpy as jnp
from jax import lax
from jax.sharding import PartitionSpec as P

NEIGHBOUR_SLOTS = 72
RBF = 16
ORBITAL_COUNT = 13
FILTER = 3


cutoff = 8.0
onsite_scale = 0.15

f32 = jnp.float32
bf16 = jnp.bfloat16


def shifted(value, axis, steps):
    count = lax.axis_size(axis)
    pairs = [(source, (source + steps) % count) for source in range(count)]
    return lax.ppermute(value, axis, pairs)


def bf16_parts(value):
    high = lax.reduce_precision(value, exponent_bits=8, mantissa_bits=7)
    rest = value - high
    middle = lax.reduce_precision(rest, exponent_bits=8, mantissa_bits=7)
    low = rest - middle
    return high.astype(bf16), middle.astype(bf16), low.astype(bf16)


def halo(flat):
    from_west = shifted(flat, "gx", 1)
    from_east = shifted(flat, "gx", -1)
    strip = jnp.stack([from_west, flat, from_east]).reshape(-1)
    from_south = shifted(strip, "gy", 1).reshape(3, -1)
    from_north = shifted(strip, "gy", -1).reshape(3, -1)
    strip = strip.reshape(3, -1)
    return jnp.stack([from_south, strip, from_north], axis=1).reshape(9, -1)


def first_halo(common, pairs):
    n = common.shape[0]
    m = pairs.shape[1]
    to_east = jnp.concatenate([common, pairs[6:9].reshape(-1)])
    to_west = jnp.concatenate([common, pairs[0:3].reshape(-1)])
    from_west = shifted(to_east, "gx", 1)
    from_east = shifted(to_west, "gx", -1)
    strip_common = jnp.stack([from_west[:n], common, from_east[:n]])
    strip_pairs = jnp.stack(
        [
            from_west[n:].reshape(3, m),
            pairs[3:6],
            from_east[n:].reshape(3, m),
        ]
    )
    to_north = jnp.concatenate([strip_common.reshape(-1), strip_pairs[:, 2].reshape(-1)])
    to_south = jnp.concatenate([strip_common.reshape(-1), strip_pairs[:, 0].reshape(-1)])
    from_south = shifted(to_north, "gy", 1)
    from_north = shifted(to_south, "gy", -1)
    all_common = jnp.stack(
        [from_south[: 3 * n].reshape(3, n), strip_common, from_north[: 3 * n].reshape(3, n)],
        axis=1,
    ).reshape(9, n)
    incoming = jnp.stack(
        [
            from_south[3 * n :].reshape(3, m),
            strip_pairs[:, 1],
            from_north[3 * n :].reshape(3, m),
        ],
        axis=1,
    ).reshape(9, m)
    return strip_common, strip_pairs[:, 1], all_common, incoming


def pair_mixed(before_rows, distance, live_flags, radial_weight, mixing_weight, gate_weight):
    centres = cutoff * jnp.arange(RBF, dtype=f32) / (RBF - 1)
    spacing = cutoff / (RBF - 1)
    basis = jnp.exp(-jnp.square((distance[:, None] - centres[None, :]) / spacing)).astype(bf16)
    cutoff_envelope = jnp.square(1.0 - jnp.square(distance / cutoff))
    before = before_rows + jnp.dot(basis, radial_weight, preferred_element_type=f32)
    edge = jax.nn.silu(before).astype(bf16)
    opened = jax.nn.silu(jnp.dot(edge, mixing_weight, preferred_element_type=f32))
    mixed = (opened * jnp.dot(edge, gate_weight, preferred_element_type=f32)).astype(bf16)
    scale_factor = 1.5 / math.sqrt(NEIGHBOUR_SLOTS * ORBITAL_COUNT) * cutoff_envelope * live_flags
    return mixed, scale_factor


def on_device(
    features,
    atom_kinds,
    kind_table,
    band_vectors,
    pair_offsets,
    pair_source,
    pair_target,
    pair_live_mask,
    radial_weight,
    w_source,
    w_target,
    mixing_weight,
    gate_weight,
    output_weight,
    w_site,
):
    atom_count = features.shape[2]
    feat = features.shape[3]
    vec = band_vectors.shape[4]
    orb = ORBITAL_COUNT
    slots = pair_source.shape[3]
    kind_hot = (
        atom_kinds[0, 0][:, None] == jnp.arange(kind_table.shape[0], dtype=jnp.int32)[None, :]
    ).astype(f32)
    embedded = jnp.dot(kind_hot, kind_table, precision=lax.Precision.HIGHEST)
    atoms = (features[0, 0].astype(f32) + embedded).astype(bf16)

    offsets = pair_offsets[0, 0]
    distance = jnp.sqrt(offsets[0] * offsets[0] + offsets[1] * offsets[1] + offsets[2] * offsets[2])
    source = pair_source[0, 0]
    target = pair_target[0, 0]
    live = pair_live_mask[0, 0]
    high, middle, low = bf16_parts(distance)
    pair_data = jnp.stack(
        [source.astype(bf16), target.astype(bf16), live.astype(bf16), high, middle, low], axis=1
    ).reshape(9, 6 * slots)

    common = jnp.concatenate([atoms.reshape(-1), band_vectors[0, 0].reshape(-1)])
    strip_common, strip_incoming, all_common, incoming = first_halo(common, pair_data)
    n_atoms = atom_count * feat
    ring_atoms = all_common[:, :n_atoms].reshape(9 * atom_count, feat)
    ring_first = all_common[:, n_atoms:]
    strip_atoms = strip_common[:, :n_atoms].reshape(3 * atom_count, feat)

    def unpack(received):
        received = received.reshape(-1, 6, slots).astype(f32)
        got_distance = (received[:, 3] + received[:, 4]) + received[:, 5]
        return (
            received[:, 0].astype(jnp.int32),
            received[:, 1].astype(jnp.int32),
            received[:, 2],
            got_distance,
        )

    def rest(values):
        return jnp.concatenate([values[0::3], values[2::3]])

    ring = 9 * atom_count
    weight_blocks = output_weight.reshape(feat, orb, orb)
    own_weight = jnp.swapaxes(weight_blocks, 1, 2).reshape(feat, orb * orb)

    def group_blocks(table_atoms, own_index, in_index, own_sets, in_sets):
        own_source, own_target, own_live, own_distance = own_sets
        in_source, in_target, in_live, in_distance = in_sets
        width = table_atoms.shape[0]
        centre_index = atom_count * (width // (2 * atom_count))
        row_source = jnp.concatenate(
            [(centre_index + own_source).reshape(-1), (in_index + in_source).reshape(-1)]
        )
        row_target = jnp.concatenate(
            [(own_index + own_target).reshape(-1), (centre_index + in_target).reshape(-1)]
        )
        group_distance = jnp.concatenate([own_distance.reshape(-1), in_distance.reshape(-1)])
        group_live = jnp.concatenate([own_live.reshape(-1), in_live.reshape(-1)])
        source_projection = jnp.dot(table_atoms, w_source, preferred_element_type=f32)
        target_projection = jnp.dot(table_atoms, w_target, preferred_element_type=f32)
        table = jnp.concatenate([source_projection, target_projection])
        table_parts = jnp.concatenate(bf16_parts(table), axis=1)
        columns = jnp.arange(2 * width, dtype=jnp.int32)[None, :]
        pick = (
            (columns == row_source[:, None]) | (columns == (row_target[:, None] + width))
        ).astype(bf16)
        picked = jnp.dot(pick, table_parts, preferred_element_type=f32)
        before_rows = (picked[:, :feat] + picked[:, feat : 2 * feat]) + picked[:, 2 * feat :]
        mixed, scale = pair_mixed(
            before_rows, group_distance, group_live, radial_weight, mixing_weight, gate_weight
        )
        own_count = own_source.size
        own_raw = jnp.einsum("fb,sf->bs", own_weight, mixed[:own_count], preferred_element_type=f32)
        in_raw = jnp.einsum("fb,sf->bs", output_weight, mixed[own_count:], preferred_element_type=f32)
        return (jnp.concatenate([own_raw, in_raw], axis=1) * scale[None, :]).astype(bf16)

    live_f = live.astype(f32)
    strip_sets = (source[1::3], target[1::3], live_f[1::3], distance[1::3])
    strip_in = unpack(strip_incoming)
    three = jnp.arange(3, dtype=jnp.int32)[:, None] * atom_count
    strip_blocks = group_blocks(strip_atoms, three, three, strip_sets, strip_in)

    rest_sets = (rest(source), rest(target), rest(live_f), rest(distance))
    rest_in = unpack(rest(incoming))
    rest_places = rest(jnp.arange(9, dtype=jnp.int32))[:, None] * atom_count
    rest_blocks = group_blocks(ring_atoms, rest_places, rest_places, rest_sets, rest_in)

    square = jnp.dot(atoms, w_site, preferred_element_type=f32).reshape(-1, orb, orb)
    onsite = (onsite_scale * 0.5 * (square + jnp.swapaxes(square, 1, 2))).astype(bf16)
    onsite_t = jnp.transpose(onsite, (2, 1, 0)).reshape(orb * orb, atom_count)
    blocks_t = jnp.concatenate([strip_blocks, rest_blocks, onsite_t], axis=1)

    own_atoms = jnp.arange(atom_count, dtype=jnp.int32)
    strip_places = jnp.array([1, 4, 7], jnp.int32)[:, None] * atom_count
    centre = 4 * atom_count
    row_atom = jnp.concatenate(
        [
            strip_sets[0].reshape(-1),
            strip_in[1].reshape(-1),
            rest_sets[0].reshape(-1),
            rest_in[1].reshape(-1),
            own_atoms,
        ]
    )
    column_atom = jnp.concatenate(
        [
            (strip_places + strip_sets[1]).reshape(-1),
            (strip_places + strip_in[0]).reshape(-1),
            (rest_places + rest_sets[1]).reshape(-1),
            (rest_places + rest_in[0]).reshape(-1),
            centre + own_atoms,
        ]
    )
    row_hot = (own_atoms[:, None] == row_atom[None, :]).astype(bf16)
    spread = (blocks_t[:, None, :] * row_hot[None, :, :]).reshape(orb * orb * atom_count, -1)
    column_hot = (column_atom[:, None] == jnp.arange(ring, dtype=jnp.int32)[None, :]).astype(bf16)
    dense = jnp.dot(spread, column_hot, preferred_element_type=f32).reshape(
        orb, orb * atom_count, ring
    )
    dense_parts = dense.astype(bf16)

    def apply(ring_vectors):
        by_orbital = jnp.swapaxes(ring_vectors.reshape(9, orb, atom_count, vec), 0, 1).reshape(
            orb, ring, vec
        )
        out = jnp.einsum("qak,qkv->qav", dense_parts, by_orbital, preferred_element_type=f32)
        return out.sum(axis=0).reshape(orb, atom_count, vec)

    first = jnp.transpose(band_vectors[0, 0], (1, 0, 2))
    previous = first.astype(f32)
    ring_first = jnp.transpose(
        ring_first.reshape(9, atom_count, orb, vec), (0, 2, 1, 3)
    ).reshape(9, -1)
    current = apply(ring_first)
    for repeat in range(FILTER - 1):
        ring_now = halo(current.astype(bf16).reshape(-1))
        upcoming = 2.0 * apply(ring_now) - previous
        previous, current = (current, upcoming)
    current = jnp.transpose(current, (1, 0, 2))
    return current[None, None]


def solution(mesh):
    in_specs = (
        P("gx", "gy", None, None),
        P("gx", "gy", None),
        P(),
        P("gx", "gy", None, None, None),
        P("gx", "gy", None, None, None),
        P("gx", "gy", None, None),
        P("gx", "gy", None, None),
        P("gx", "gy", None, None),
        P(),
        P(),
        P(),
        P(),
        P(),
        P(),
        P(),
    )
    out_specs = P("gx", "gy", None, None, None)
    return jax.shard_map(
        on_device, mesh=mesh, in_specs=in_specs, out_specs=out_specs, check_vma=False
    )
```

```python
import math

import jax
import jax.numpy as jnp
from jax import lax
from jax.sharding import PartitionSpec as P

NEIGHBOUR_SLOTS = 72
RBF = 16
ORBITAL_COUNT = 13
FILTER = 3


cutoff = 8.0
onsite_scale = 0.15

f32 = jnp.float32
bf16 = jnp.bfloat16


def shifted(value, axis, steps):
    count = lax.axis_size(axis)
    pairs = [(source, (source + steps) % count) for source in range(count)]
    return lax.ppermute(value, axis, pairs)


def bf16_parts(value):
    high = lax.reduce_precision(value, exponent_bits=8, mantissa_bits=7)
    rest = value - high
    middle = lax.reduce_precision(rest, exponent_bits=8, mantissa_bits=7)
    low = rest - middle
    return high.astype(bf16), middle.astype(bf16), low.astype(bf16)


def halo(flat):
    from_west = shifted(flat, "gx", 1)
    from_east = shifted(flat, "gx", -1)
    strip = jnp.stack([from_west, flat, from_east]).reshape(-1)
    from_south = shifted(strip, "gy", 1).reshape(3, -1)
    from_north = shifted(strip, "gy", -1).reshape(3, -1)
    strip = strip.reshape(3, -1)
    return jnp.stack([from_south, strip, from_north], axis=1).reshape(9, -1)


def first_halo(common, pairs):
    n = common.shape[0]
    m = pairs.shape[1]
    to_east = jnp.concatenate([common, pairs[6:9].reshape(-1)])
    to_west = jnp.concatenate([common, pairs[0:3].reshape(-1)])
    from_west = shifted(to_east, "gx", 1)
    from_east = shifted(to_west, "gx", -1)
    strip_common = jnp.stack([from_west[:n], common, from_east[:n]])
    strip_pairs = jnp.stack(
        [
            from_west[n:].reshape(3, m),
            pairs[3:6],
            from_east[n:].reshape(3, m),
        ]
    )
    to_north = jnp.concatenate([strip_common.reshape(-1), strip_pairs[:, 2].reshape(-1)])
    to_south = jnp.concatenate([strip_common.reshape(-1), strip_pairs[:, 0].reshape(-1)])
    from_south = shifted(to_north, "gy", 1)
    from_north = shifted(to_south, "gy", -1)
    all_common = jnp.stack(
        [from_south[: 3 * n].reshape(3, n), strip_common, from_north[: 3 * n].reshape(3, n)],
        axis=1,
    ).reshape(9, n)
    incoming = jnp.stack(
        [
            from_south[3 * n :].reshape(3, m),
            strip_pairs[:, 1],
            from_north[3 * n :].reshape(3, m),
        ],
        axis=1,
    ).reshape(9, m)
    return strip_common, strip_pairs[:, 1], all_common, incoming


def pair_mixed(before_rows, distance, live_flags, radial_weight, mixing_weight, gate_weight):
    centres = cutoff * jnp.arange(RBF, dtype=f32) / (RBF - 1)
    spacing = cutoff / (RBF - 1)
    basis = jnp.exp(-jnp.square((distance[:, None] - centres[None, :]) / spacing)).astype(bf16)
    cutoff_envelope = jnp.square(1.0 - jnp.square(distance / cutoff))
    before = before_rows + jnp.dot(basis, radial_weight, preferred_element_type=f32)
    edge = jax.nn.silu(before).astype(bf16)
    opened = jax.nn.silu(jnp.dot(edge, mixing_weight, preferred_element_type=f32))
    mixed = (opened * jnp.dot(edge, gate_weight, preferred_element_type=f32)).astype(bf16)
    scale_factor = 1.5 / math.sqrt(NEIGHBOUR_SLOTS * ORBITAL_COUNT) * cutoff_envelope * live_flags
    return mixed, scale_factor


def on_device(
    features,
    atom_kinds,
    kind_table,
    band_vectors,
    pair_offsets,
    pair_source,
    pair_target,
    pair_live_mask,
    radial_weight,
    w_source,
    w_target,
    mixing_weight,
    gate_weight,
    output_weight,
    w_site,
):
    atom_count = features.shape[2]
    feat = features.shape[3]
    vec = band_vectors.shape[4]
    orb = ORBITAL_COUNT
    slots = pair_source.shape[3]
    kinds = atom_kinds[0, 0][:, None]
    embedded = jnp.zeros((atom_count, feat), f32)
    for kind in range(kind_table.shape[0]):
        embedded = jnp.where(kinds == kind, kind_table[kind][None, :], embedded)
    atoms = (features[0, 0].astype(f32) + embedded).astype(bf16)

    offsets = pair_offsets[0, 0]
    distance = jnp.sqrt(offsets[0] * offsets[0] + offsets[1] * offsets[1] + offsets[2] * offsets[2])
    source = pair_source[0, 0]
    target = pair_target[0, 0]
    live = pair_live_mask[0, 0]
    high, middle, low = bf16_parts(distance)
    pair_data = jnp.stack(
        [source.astype(bf16), target.astype(bf16), live.astype(bf16), high, middle, low], axis=1
    ).reshape(9, 6 * slots)

    common = jnp.concatenate([atoms.reshape(-1), band_vectors[0, 0].reshape(-1)])
    strip_common, strip_incoming, all_common, incoming = first_halo(common, pair_data)
    n_atoms = atom_count * feat
    ring_atoms = all_common[:, :n_atoms].reshape(9 * atom_count, feat)
    ring_first = all_common[:, n_atoms:]
    strip_atoms = strip_common[:, :n_atoms].reshape(3 * atom_count, feat)

    def unpack(received):
        received = received.reshape(-1, 6, slots).astype(f32)
        got_distance = (received[:, 3] + received[:, 4]) + received[:, 5]
        return (
            received[:, 0].astype(jnp.int32),
            received[:, 1].astype(jnp.int32),
            received[:, 2],
            got_distance,
        )

    def rest(values):
        return jnp.concatenate([values[0::3], values[2::3]])

    ring = 9 * atom_count
    weight_blocks = output_weight.reshape(feat, orb, orb)
    own_weight = jnp.swapaxes(weight_blocks, 1, 2).reshape(feat, orb * orb)

    def group_blocks(table_atoms, own_index, in_index, own_sets, in_sets):
        own_source, own_target, own_live, own_distance = own_sets
        in_source, in_target, in_live, in_distance = in_sets
        width = table_atoms.shape[0]
        centre_index = atom_count * (width // (2 * atom_count))
        row_source = jnp.concatenate(
            [(centre_index + own_source).reshape(-1), (in_index + in_source).reshape(-1)]
        )
        row_target = jnp.concatenate(
            [(own_index + own_target).reshape(-1), (centre_index + in_target).reshape(-1)]
        )
        group_distance = jnp.concatenate([own_distance.reshape(-1), in_distance.reshape(-1)])
        group_live = jnp.concatenate([own_live.reshape(-1), in_live.reshape(-1)])
        source_projection = jnp.dot(table_atoms, w_source, preferred_element_type=f32)
        target_projection = jnp.dot(table_atoms, w_target, preferred_element_type=f32)
        table = jnp.concatenate([source_projection, target_projection])
        table_parts = jnp.concatenate(bf16_parts(table), axis=1)
        columns = jnp.arange(2 * width, dtype=jnp.int32)[None, :]
        pick = (
            (columns == row_source[:, None]) | (columns == (row_target[:, None] + width))
        ).astype(bf16)
        picked = jnp.dot(pick, table_parts, preferred_element_type=f32)
        before_rows = (picked[:, :feat] + picked[:, feat : 2 * feat]) + picked[:, 2 * feat :]
        mixed, scale = pair_mixed(
            before_rows, group_distance, group_live, radial_weight, mixing_weight, gate_weight
        )
        own_count = own_source.size
        own_raw = jnp.einsum("fb,sf->bs", own_weight, mixed[:own_count], preferred_element_type=f32)
        in_raw = jnp.einsum("fb,sf->bs", output_weight, mixed[own_count:], preferred_element_type=f32)
        return (jnp.concatenate([own_raw, in_raw], axis=1) * scale[None, :]).astype(bf16)

    live_f = live.astype(f32)
    strip_sets = (source[1::3], target[1::3], live_f[1::3], distance[1::3])
    strip_in = unpack(strip_incoming)
    three = jnp.arange(3, dtype=jnp.int32)[:, None] * atom_count
    strip_blocks = group_blocks(strip_atoms, three, three, strip_sets, strip_in)

    rest_sets = (rest(source), rest(target), rest(live_f), rest(distance))
    rest_in = unpack(rest(incoming))
    rest_places = rest(jnp.arange(9, dtype=jnp.int32))[:, None] * atom_count
    rest_blocks = group_blocks(ring_atoms, rest_places, rest_places, rest_sets, rest_in)

    square = jnp.dot(atoms, w_site, preferred_element_type=f32).reshape(-1, orb, orb)
    onsite = (onsite_scale * 0.5 * (square + jnp.swapaxes(square, 1, 2))).astype(bf16)
    onsite_t = jnp.transpose(onsite, (2, 1, 0)).reshape(orb * orb, atom_count)
    blocks_t = jnp.concatenate([strip_blocks, rest_blocks, onsite_t], axis=1)

    own_atoms = jnp.arange(atom_count, dtype=jnp.int32)
    strip_places = jnp.array([1, 4, 7], jnp.int32)[:, None] * atom_count
    centre = 4 * atom_count
    row_atom = jnp.concatenate(
        [
            strip_sets[0].reshape(-1),
            strip_in[1].reshape(-1),
            rest_sets[0].reshape(-1),
            rest_in[1].reshape(-1),
            own_atoms,
        ]
    )
    column_atom = jnp.concatenate(
        [
            (strip_places + strip_sets[1]).reshape(-1),
            (strip_places + strip_in[0]).reshape(-1),
            (rest_places + rest_sets[1]).reshape(-1),
            (rest_places + rest_in[0]).reshape(-1),
            centre + own_atoms,
        ]
    )
    row_hot = (own_atoms[:, None] == row_atom[None, :]).astype(bf16)
    spread = (blocks_t[:, None, :] * row_hot[None, :, :]).reshape(orb * orb * atom_count, -1)
    column_hot = (column_atom[:, None] == jnp.arange(ring, dtype=jnp.int32)[None, :]).astype(bf16)
    dense = jnp.dot(spread, column_hot, preferred_element_type=f32).reshape(
        orb, orb * atom_count, ring
    )
    dense_parts = dense.astype(bf16)

    def apply(ring_vectors):
        by_orbital = jnp.swapaxes(ring_vectors.reshape(9, orb, atom_count, vec), 0, 1).reshape(
            orb, ring, vec
        )
        out = jnp.einsum("qak,qkv->qav", dense_parts, by_orbital, preferred_element_type=f32)
        return out.sum(axis=0).reshape(orb, atom_count, vec)

    first = jnp.transpose(band_vectors[0, 0], (1, 0, 2))
    previous = first.astype(f32)
    ring_first = jnp.transpose(
        ring_first.reshape(9, atom_count, orb, vec), (0, 2, 1, 3)
    ).reshape(9, -1)
    current = apply(ring_first)
    for repeat in range(FILTER - 1):
        ring_now = halo(current.astype(bf16).reshape(-1))
        upcoming = 2.0 * apply(ring_now) - previous
        previous, current = (current, upcoming)
    current = jnp.transpose(current, (1, 0, 2))
    return current[None, None]


def solution(mesh):
    in_specs = (
        P("gx", "gy", None, None),
        P("gx", "gy", None),
        P(),
        P("gx", "gy", None, None, None),
        P("gx", "gy", None, None, None),
        P("gx", "gy", None, None),
        P("gx", "gy", None, None),
        P("gx", "gy", None, None),
        P(),
        P(),
        P(),
        P(),
        P(),
        P(),
        P(),
    )
    out_specs = P("gx", "gy", None, None, None)
    return jax.shard_map(
        on_device, mesh=mesh, in_specs=in_specs, out_specs=out_specs, check_vma=False
    )
```
